32 devices in a mesh: pair: 1, contr: 32 (over z, y, x, core).
Axes of the slice: x: 2, y: 2, z: 4, core: 2. Of those that a mesh axis runs over, the one named last changes fastest.
Arguments:
- amplitudes: bfloat16 [1024, 32768], P('pair', 'contr'), may hold values from -6 to 6
- integrals: bfloat16 [32768, 256], P('contr', 'pair'), may hold values from -0.09375 to 0.09375
- occ_irrep: int32 [64], replicated, may hold values from 0 to 7
- virt_irrep: int32 [512], replicated, may hold values from 0 to 7
- occ_energy: float32 [64], replicated, may hold values from -2 to -0.5
- virt_energy: float32 [512], replicated, may hold values from 0.5 to 3
- slab_start: int32 [2], replicated, may hold values from 0 to 496
Outputs:
- update: bfloat16 [1024, 256], P(('pair', 'contr'))
The draws below stay inside these ranges and needn't reach their ends.
All inputs are finite; a program needn't handle non-finite values.
Results may differ from the reference program's by a relative error of at most 0.003.
Values may be sent and summed in bfloat16 or wider, within the bound.
No kernel may reach another device: no remote copies, remote signals or barrier semaphores. Data moves between devices by JAX's collectives and lax.ppermute only.
A program may use at most 64 MiB of HBM per device.

```python
import jax
import jax.numpy as jnp
from jax import lax

VIRT = 512
SLAB = 16
BSLAB = 4
OCC = 64
ROWS = 1024
COLS = 256
KC = 32768


def plant(result, key, smallest, high):
    longest = result.shape.index(max(result.shape))
    spots = []
    for shift in (0, 1):
        where = [jax.random.randint(jax.random.fold_in(key, axis), (), 0, length) for axis, length in enumerate(result.shape)]
        where[longest] = (where[longest] + shift) % result.shape[longest]
        spots.append(tuple(where))
    return result.at[spots[0]].set(smallest).at[spots[1]].set(high)


def raised(entries, own_key, source, target, parts, factor):
    owner, partner = [(jnp.arange(entries.shape[position]) // (entries.shape[position] // parts)).reshape([-1 if axis == position else 1 for axis in range(entries.ndim)]) for position in (source, target)]
    chosen = jax.random.permutation(own_key, parts)[partner]
    strong = (owner == chosen) | (owner == (partner + parts // 2) % parts)
    return jnp.where(strong, factor * entries, entries)


def block_levels(own_key, shape, cuts, least, high):
    def one(axis_at, blocks):
        steps = jax.random.uniform(jax.random.fold_in(jax.random.fold_in(own_key, 6), axis_at), (blocks,), jnp.float32, least / len(cuts), high / len(cuts))
        return jnp.repeat(jnp.exp(steps), shape[axis_at] // blocks).reshape((-1,) + (1,) * (len(shape) - axis_at - 1))

    loudness = one(*cuts[0])
    for cut in cuts[1:]:
        loudness = loudness * one(*cut)
    return loudness


def bell_draw(rng, dims, width, most, pieces=(), kind=jnp.bfloat16):
    entries = width * jax.random.normal(rng, dims, jnp.float32)
    if pieces:
        entries = entries * block_levels(rng, dims, pieces, -0.22, 0.18)
    return jnp.clip(entries, -most, most).astype(kind)


def bell_draw_with(own_key, dims, scale, reach, pieces, heavy, held_as=jnp.bfloat16):
    result = scale * jax.random.normal(own_key, dims, jnp.float32)
    if pieces:
        result = result * block_levels(own_key, dims, pieces, -0.22, 0.18)
    return jnp.clip(raised(result, jax.random.fold_in(own_key, 3), *heavy), -reach, reach).astype(held_as)


def setup_inputs(seed: int = 0) -> dict:
    streams_of = jax.random.split(jax.random.key(seed), 8)
    amplitudes = bell_draw_with(streams_of[0], (ROWS, KC), 1.0, 6.0, ((1, 32),), (1, 0, 32, 2.75))
    integrals = bell_draw(streams_of[1], (KC, COLS), (KC // 8) ** -0.5, 0.09375, ((0, 32),))
    occ_irrep = plant(jax.random.randint(streams_of[2], (OCC,), 0, 8), jax.random.fold_in(streams_of[2], 1), 0, 7).astype(jnp.int32)
    virt_irrep = plant(jax.random.randint(streams_of[3], (VIRT,), 0, 8), jax.random.fold_in(streams_of[3], 1), 0, 7).astype(jnp.int32)
    occ_energy = jnp.clip(jax.random.uniform(streams_of[4], (OCC,), jnp.float32, -2.0, -0.5), -2.0, -0.5)
    virt_energy = jnp.clip(jax.random.uniform(streams_of[5], (VIRT,), jnp.float32, 0.5, 3.0), 0.5, 3.0)
    slab_start = jax.random.randint(streams_of[6], (2,), 0, VIRT - max(SLAB, BSLAB) + 1).astype(jnp.int32)
    return {"amplitudes": amplitudes, "integrals": integrals, "occ_irrep": occ_irrep, "virt_irrep": virt_irrep, "occ_energy": occ_energy, "virt_energy": virt_energy, "slab_start": slab_start}


def reference(amplitudes, integrals, occ_irrep, virt_irrep, occ_energy, virt_energy, slab_start):
    first_start = slab_start[0].astype(jnp.int32)
    second_start = slab_start[1].astype(jnp.int32)
    a_irrep = lax.dynamic_slice(virt_irrep, (first_start,), (SLAB,))
    b_irrep = lax.dynamic_slice(virt_irrep, (second_start,), (BSLAB,))
    a_energy = lax.dynamic_slice(virt_energy, (first_start,), (SLAB,))
    b_energy = lax.dynamic_slice(virt_energy, (second_start,), (BSLAB,))
    row_irrep = jnp.bitwise_xor(occ_irrep[:, None], a_irrep[None, :]).reshape(-1)
    col_irrep = jnp.bitwise_xor(occ_irrep[:, None], b_irrep[None, :]).reshape(-1)
    row_energy = (occ_energy[:, None] - a_energy[None, :]).reshape(-1)
    col_energy = (occ_energy[:, None] - b_energy[None, :]).reshape(-1)
    zero = jnp.zeros((), jnp.bfloat16)

    def add_block(occupied, total):
        offset = (occupied * VIRT).astype(jnp.int32)
        kc_irrep = jnp.bitwise_xor(occ_irrep[occupied], virt_irrep)
        amp_block = lax.dynamic_slice(amplitudes, (jnp.int32(0), offset), (ROWS, VIRT))
        int_block = lax.dynamic_slice(integrals, (offset, jnp.int32(0)), (VIRT, COLS))
        amp_masked = jnp.where(row_irrep[:, None] == kc_irrep[None, :], amp_block, zero)
        int_masked = jnp.where(kc_irrep[:, None] == col_irrep[None, :], int_block, zero)
        return total + jnp.dot(amp_masked, int_masked, preferred_element_type=jnp.float32)

    cycle = lax.fori_loop(0, OCC, add_block, jnp.zeros((ROWS, COLS), jnp.float32))
    denominator = row_energy[:, None] + col_energy[None, :]
    return (cycle / denominator).astype(jnp.bfloat16)
```

```python
import jax
import jax.numpy as jnp
from jax import lax
from jax.sharding import PartitionSpec as P


def halving_scatter(partial, axis, count, index):
    rows, cols = partial.shape
    block = rows // count
    buf = partial.reshape(count, block, cols)
    stage = 0
    while (1 << stage) < count:
        half = buf.shape[0] // 2
        pairs = buf.reshape(half, 2, block, cols)
        bit = (index >> stage) & 1
        keep = lax.dynamic_index_in_dim(pairs, bit, axis=1, keepdims=False)
        send = lax.dynamic_index_in_dim(pairs, 1 - bit, axis=1, keepdims=False)
        perm = [(i, i ^ (1 << stage)) for i in range(count)]
        buf = keep + lax.ppermute(send, axis, perm)
        stage += 1
    return buf.reshape(block, cols)


def body(amplitudes, integrals, occ_irrep, virt_irrep, occ_energy, virt_energy, slab_start):
    pair_count = lax.axis_size("pair")
    contr_count = lax.axis_size("contr")
    pair_index = lax.axis_index("pair")
    contr_index = lax.axis_index("contr")
    virt_count = virt_irrep.shape[0]
    kc_local = integrals.shape[0]
    occ_local = kc_local // virt_count
    rows_pair = amplitudes.shape[0]
    cols_pair = integrals.shape[1]
    rows_device = rows_pair // contr_count
    slab_first = amplitudes.shape[0] * pair_count // occ_irrep.shape[0]
    slab_second = cols_pair * pair_count // occ_irrep.shape[0]
    first_start = slab_start[0]
    second_start = slab_start[1]
    a_irrep = lax.dynamic_slice(virt_irrep, (first_start,), (slab_first,))
    b_irrep = lax.dynamic_slice(virt_irrep, (second_start,), (slab_second,))
    a_energy = lax.dynamic_slice(virt_energy, (first_start,), (slab_first,))
    b_energy = lax.dynamic_slice(virt_energy, (second_start,), (slab_second,))
    row_irrep = jnp.bitwise_xor(occ_irrep[:, None], a_irrep[None, :]).reshape(-1)
    col_irrep = jnp.bitwise_xor(occ_irrep[:, None], b_irrep[None, :]).reshape(-1)
    row_energy = (occ_energy[:, None] - a_energy[None, :]).reshape(-1)
    col_energy = (occ_energy[:, None] - b_energy[None, :]).reshape(-1)
    local_occ = lax.dynamic_slice(occ_irrep, (contr_index * occ_local,), (occ_local,))
    kc_irrep = jnp.bitwise_xor(local_occ[:, None], virt_irrep[None, :]).reshape(-1)
    zero = jnp.zeros((), jnp.bfloat16)
    whole_int = lax.all_gather(integrals, "pair", axis=1, tiled=True)
    int_masked = jnp.where(kc_irrep[:, None] == col_irrep[None, :], whole_int, zero)
    row_irrep_pair = lax.dynamic_slice(row_irrep, (pair_index * rows_pair,), (rows_pair,))
    amp_masked = jnp.where(row_irrep_pair[:, None] == kc_irrep[None, :], amplitudes, zero)
    partial = jnp.dot(amp_masked, int_masked, preferred_element_type=jnp.float32)
    if contr_count & (contr_count - 1) == 0 and rows_pair % contr_count == 0:
        summed = halving_scatter(partial, "contr", contr_count, contr_index)
    else:
        summed = lax.psum_scatter(partial, "contr", scatter_dimension=0, tiled=True)
    mine_energy = lax.dynamic_slice(
        row_energy, (pair_index * rows_pair + contr_index * rows_device,), (rows_device,)
    )
    update = (summed / (mine_energy[:, None] + col_energy[None, :])).astype(jnp.bfloat16)
    return update


def solution(mesh):
    in_specs = (P("pair", "contr"), P("contr", "pair"), P(), P(), P(), P(), P())
    out_specs = P(("pair", "contr"), None)
    return jax.shard_map(body, mesh=mesh, in_specs=in_specs, out_specs=out_specs, check_vma=False)
```

```python
import jax
import jax.numpy as jnp
from jax import lax
from jax.sharding import PartitionSpec as P


def halving_scatter(partial, axis, count, index):
    rows, cols = partial.shape
    block = rows // count
    bits = count.bit_length() - 1
    first = (index & 1) == 0

    def order(c):
        seq = list(range(bits))
        if c == 1 and bits >= 3:
            seq[1], seq[2] = seq[2], seq[1]
        return seq

    buf = partial.reshape((2,) * bits + (block, cols))
    left = [list(range(bits - 1, -1, -1)) for _ in range(2)]
    for stage in range(bits):
        split = [order(c)[stage] for c in range(2)]
        where = [left[c].index(split[c]) for c in range(2)]
        mine = [(index >> split[c]) & 1 for c in range(2)]
        if where[0] == where[1]:
            bit = jnp.where(first, mine[0], mine[1]) if split[0] != split[1] else mine[0]
            keep = lax.dynamic_index_in_dim(buf, bit, axis=where[0], keepdims=False)
            send = lax.dynamic_index_in_dim(buf, 1 - bit, axis=where[0], keepdims=False)
        else:
            picks = [
                [lax.dynamic_index_in_dim(buf, v, axis=where[c], keepdims=False)
                 for v in (mine[c], 1 - mine[c])]
                for c in range(2)
            ]
            keep = jnp.where(first, picks[0][0], picks[1][0])
            send = jnp.where(first, picks[0][1], picks[1][1])
        for c in range(2):
            left[c].pop(where[c])
        perm = [(i, i ^ (1 << order(i & 1)[stage])) for i in range(count)]
        buf = keep + lax.ppermute(send, axis, perm)
    return buf.reshape(block, cols)


def body(amplitudes, integrals, occ_irrep, virt_irrep, occ_energy, virt_energy, slab_start):
    pair_count = lax.axis_size("pair")
    contr_count = lax.axis_size("contr")
    pair_index = lax.axis_index("pair")
    contr_index = lax.axis_index("contr")
    virt_count = virt_irrep.shape[0]
    kc_local = integrals.shape[0]
    occ_local = kc_local // virt_count
    rows_pair = amplitudes.shape[0]
    cols_pair = integrals.shape[1]
    rows_device = rows_pair // contr_count
    slab_first = amplitudes.shape[0] * pair_count // occ_irrep.shape[0]
    slab_second = cols_pair * pair_count // occ_irrep.shape[0]
    first_start = slab_start[0]
    second_start = slab_start[1]
    a_irrep = lax.dynamic_slice(virt_irrep, (first_start,), (slab_first,))
    b_irrep = lax.dynamic_slice(virt_irrep, (second_start,), (slab_second,))
    a_energy = lax.dynamic_slice(virt_energy, (first_start,), (slab_first,))
    b_energy = lax.dynamic_slice(virt_energy, (second_start,), (slab_second,))
    row_irrep = jnp.bitwise_xor(occ_irrep[:, None], a_irrep[None, :]).reshape(-1)
    col_irrep = jnp.bitwise_xor(occ_irrep[:, None], b_irrep[None, :]).reshape(-1)
    row_energy = (occ_energy[:, None] - a_energy[None, :]).reshape(-1)
    col_energy = (occ_energy[:, None] - b_energy[None, :]).reshape(-1)
    local_occ = lax.dynamic_slice(occ_irrep, (contr_index * occ_local,), (occ_local,))
    kc_irrep = jnp.bitwise_xor(local_occ[:, None], virt_irrep[None, :]).reshape(-1)
    zero = jnp.zeros((), jnp.bfloat16)
    whole_int = lax.all_gather(integrals, "pair", axis=1, tiled=True)
    int_masked = jnp.where(kc_irrep[:, None] == col_irrep[None, :], whole_int, zero)
    row_irrep_pair = lax.dynamic_slice(row_irrep, (pair_index * rows_pair,), (rows_pair,))
    amp_masked = jnp.where(row_irrep_pair[:, None] == kc_irrep[None, :], amplitudes, zero)
    partial = jnp.dot(amp_masked, int_masked, preferred_element_type=jnp.float32)
    if contr_count & (contr_count - 1) == 0 and rows_pair % contr_count == 0:
        summed = halving_scatter(partial, "contr", contr_count, contr_index)
    else:
        summed = lax.psum_scatter(partial, "contr", scatter_dimension=0, tiled=True)
    mine_energy = lax.dynamic_slice(
        row_energy, (pair_index * rows_pair + contr_index * rows_device,), (rows_device,)
    )
    update = (summed / (mine_energy[:, None] + col_energy[None, :])).astype(jnp.bfloat16)
    return update


def solution(mesh):
    in_specs = (P("pair", "contr"), P("contr", "pair"), P(), P(), P(), P(), P())
    out_specs = P(("pair", "contr"), None)
    return jax.shard_map(body, mesh=mesh, in_specs=in_specs, out_specs=out_specs, check_vma=False)
```

```python
import jax
import jax.numpy as jnp
from jax import lax
from jax.sharding import PartitionSpec as P


def halving_scatter(partial, axis, count, index):
    rows, cols = partial.shape
    block = rows // count
    bits = count.bit_length() - 1
    first = (index & 1) == 0

    def order(c):
        seq = list(range(bits))
        if c == 1 and bits >= 3:
            seq[1], seq[2] = seq[2], seq[1]
        return seq

    buf = partial.reshape((2,) * bits + (block, cols))
    left = [list(range(bits - 1, -1, -1)) for _ in range(2)]
    for stage in range(bits):
        split = [order(c)[stage] for c in range(2)]
        where = [left[c].index(split[c]) for c in range(2)]
        mine = [(index >> split[c]) & 1 for c in range(2)]
        if where[0] == where[1]:
            bit = jnp.where(first, mine[0], mine[1]) if split[0] != split[1] else mine[0]
            keep = lax.dynamic_index_in_dim(buf, bit, axis=where[0], keepdims=False)
            send = lax.dynamic_index_in_dim(buf, 1 - bit, axis=where[0], keepdims=False)
        else:
            picks = [
                [lax.dynamic_index_in_dim(buf, v, axis=where[c], keepdims=False)
                 for v in (mine[c], 1 - mine[c])]
                for c in range(2)
            ]
            keep = jnp.where(first, picks[0][0], picks[1][0])
            send = jnp.where(first, picks[0][1], picks[1][1])
        for c in range(2):
            left[c].pop(where[c])
        perm = [(i, i ^ (1 << order(i & 1)[stage])) for i in range(count)]
        buf = keep + lax.ppermute(send, axis, perm)
    return buf.reshape(block, cols)


def body(amplitudes, integrals, occ_irrep, virt_irrep, occ_energy, virt_energy, slab_start):
    pair_count = lax.axis_size("pair")
    contr_count = lax.axis_size("contr")
    pair_index = lax.axis_index("pair")
    contr_index = lax.axis_index("contr")
    virt_count = virt_irrep.shape[0]
    kc_local = integrals.shape[0]
    occ_local = kc_local // virt_count
    rows_pair = amplitudes.shape[0]
    cols_pair = integrals.shape[1]
    rows_device = rows_pair // contr_count
    slab_first = amplitudes.shape[0] * pair_count // occ_irrep.shape[0]
    slab_second = cols_pair * pair_count // occ_irrep.shape[0]
    first_start = slab_start[0]
    second_start = slab_start[1]
    a_irrep = lax.dynamic_slice(virt_irrep, (first_start,), (slab_first,))
    b_irrep = lax.dynamic_slice(virt_irrep, (second_start,), (slab_second,))
    a_energy = lax.dynamic_slice(virt_energy, (first_start,), (slab_first,))
    b_energy = lax.dynamic_slice(virt_energy, (second_start,), (slab_second,))
    row_irrep = jnp.bitwise_xor(occ_irrep[:, None], a_irrep[None, :]).reshape(-1)
    col_irrep = jnp.bitwise_xor(occ_irrep[:, None], b_irrep[None, :]).reshape(-1)
    row_energy = (occ_energy[:, None] - a_energy[None, :]).reshape(-1)
    col_energy = (occ_energy[:, None] - b_energy[None, :]).reshape(-1)
    local_occ = lax.dynamic_slice(occ_irrep, (contr_index * occ_local,), (occ_local,))
    kc_irrep = jnp.bitwise_xor(local_occ[:, None], virt_irrep[None, :]).reshape(-1)
    zero = jnp.zeros((), jnp.bfloat16)
    whole_int = lax.all_gather(integrals, "pair", axis=1, tiled=True)
    int_masked = jnp.where(kc_irrep[:, None] == col_irrep[None, :], whole_int, zero)
    partial = jnp.dot(amplitudes, int_masked, preferred_element_type=jnp.float32)
    if contr_count & (contr_count - 1) == 0 and rows_pair % contr_count == 0:
        summed = halving_scatter(partial, "contr", contr_count, contr_index)
    else:
        summed = lax.psum_scatter(partial, "contr", scatter_dimension=0, tiled=True)
    mine_irrep = lax.dynamic_slice(
        row_irrep, (pair_index * rows_pair + contr_index * rows_device,), (rows_device,)
    )
    summed = jnp.where(mine_irrep[:, None] == col_irrep[None, :], summed, 0.0)
    mine_energy = lax.dynamic_slice(
        row_energy, (pair_index * rows_pair + contr_index * rows_device,), (rows_device,)
    )
    update = (summed / (mine_energy[:, None] + col_energy[None, :])).astype(jnp.bfloat16)
    return update


def solution(mesh):
    in_specs = (P("pair", "contr"), P("contr", "pair"), P(), P(), P(), P(), P())
    out_specs = P(("pair", "contr"), None)
    return jax.shard_map(body, mesh=mesh, in_specs=in_specs, out_specs=out_specs, check_vma=False)
```

```python
import jax
import jax.numpy as jnp
from jax import lax
from jax.experimental import pallas as pl
from jax.experimental.pallas import tpu as pltpu
from jax.sharding import PartitionSpec as P


def halving_scatter(partial, axis, count, index):
    rows, cols = partial.shape
    block = rows // count
    bits = count.bit_length() - 1
    first = (index & 1) == 0

    def order(c):
        seq = list(range(bits))
        if c == 1 and bits >= 3:
            seq[1], seq[2] = seq[2], seq[1]
        return seq

    buf = partial.reshape((2,) * bits + (block, cols))
    left = [list(range(bits - 1, -1, -1)) for _ in range(2)]
    for stage in range(bits):
        split = [order(c)[stage] for c in range(2)]
        where = [left[c].index(split[c]) for c in range(2)]
        mine = [(index >> split[c]) & 1 for c in range(2)]
        if where[0] == where[1]:
            bit = jnp.where(first, mine[0], mine[1]) if split[0] != split[1] else mine[0]
            keep = lax.dynamic_index_in_dim(buf, bit, axis=where[0], keepdims=False)
            send = lax.dynamic_index_in_dim(buf, 1 - bit, axis=where[0], keepdims=False)
        else:
            picks = [
                [lax.dynamic_index_in_dim(buf, v, axis=where[c], keepdims=False)
                 for v in (mine[c], 1 - mine[c])]
                for c in range(2)
            ]
            keep = jnp.where(first, picks[0][0], picks[1][0])
            send = jnp.where(first, picks[0][1], picks[1][1])
        for c in range(2):
            left[c].pop(where[c])
        perm = [(i, i ^ (1 << order(i & 1)[stage])) for i in range(count)]
        buf = keep + lax.ppermute(send, axis, perm)
    return buf.reshape(block, cols)


def _masked_product_kernel(slab_ref, occ_s_ref, occ_v_ref, virt_v_ref, amp_ref, int_ref, out_ref):
    virt_count = virt_v_ref.shape[0]
    occ_count = occ_v_ref.shape[0]
    kc_local, cols = int_ref.shape
    occ_local = kc_local // virt_count
    per_occ = cols // occ_count
    second_start = slab_ref[1]
    base = lax.axis_index("contr") * occ_local
    f32, bf16 = jnp.float32, jnp.bfloat16
    occ_rows = jnp.broadcast_to(occ_v_ref[...].reshape(1, occ_count), (8, occ_count)).astype(bf16)
    virt_rows = jnp.broadcast_to(virt_v_ref[...].reshape(1, virt_count), (8, virt_count)).astype(bf16)
    q_of = lax.broadcasted_iota(jnp.int32, (occ_count, cols), 1)
    j_of = lax.broadcasted_iota(jnp.int32, (occ_count, cols), 0)
    occ_pick = (q_of // per_occ == j_of).astype(bf16)
    q_of = lax.broadcasted_iota(jnp.int32, (virt_count, cols), 1)
    c_of = lax.broadcasted_iota(jnp.int32, (virt_count, cols), 0)
    virt_pick = (c_of == second_start + q_of % per_occ).astype(bf16)
    col_occ = jnp.dot(occ_rows, occ_pick, preferred_element_type=f32)
    col_virt = jnp.dot(virt_rows, virt_pick, preferred_element_type=f32)
    col_irrep = jnp.bitwise_xor(col_occ.astype(jnp.int32), col_virt.astype(jnp.int32))[0:1, :]
    eye = (lax.broadcasted_iota(jnp.int32, (virt_count, virt_count), 0)
           == lax.broadcasted_iota(jnp.int32, (virt_count, virt_count), 1)).astype(bf16)
    virt_col = lax.dot_general(eye, virt_rows, (((1,), (1,)), ((), ())), preferred_element_type=f32)
    virt_col = virt_col.astype(jnp.int32)[:, 0:1]
    total = None
    for k in range(occ_local):
        kc_irrep = jnp.bitwise_xor(virt_col, occ_s_ref[base + k])
        block = int_ref[k * virt_count:(k + 1) * virt_count, :]
        masked = jnp.where(kc_irrep == col_irrep, block, jnp.zeros_like(block))
        term = jnp.dot(amp_ref[:, k * virt_count:(k + 1) * virt_count], masked, preferred_element_type=f32)
        total = term if total is None else total + term
    out_ref[...] = total


def masked_product(slab_start, occ_irrep, virt_irrep, amplitudes, integrals):
    rows, kc_local = amplitudes.shape
    cols = integrals.shape[1]
    smem = pl.BlockSpec(memory_space=pltpu.SMEM)
    vmem = pl.BlockSpec(memory_space=pltpu.VMEM)
    return pl.pallas_call(
        _masked_product_kernel,
        out_shape=jax.ShapeDtypeStruct((rows, cols), jnp.float32),
        in_specs=[smem, smem, vmem, vmem, vmem, vmem],
        out_specs=vmem,
        cost_estimate=pl.CostEstimate(
            flops=2 * rows * kc_local * cols,
            bytes_accessed=2 * rows * kc_local + 2 * kc_local * cols + 4 * rows * cols,
            transcendentals=0,
        ),
    )(slab_start, occ_irrep, occ_irrep, virt_irrep, amplitudes, integrals)


def body(amplitudes, integrals, occ_irrep, virt_irrep, occ_energy, virt_energy, slab_start):
    pair_count = lax.axis_size("pair")
    contr_count = lax.axis_size("contr")
    pair_index = lax.axis_index("pair")
    contr_index = lax.axis_index("contr")
    virt_count = virt_irrep.shape[0]
    kc_local = integrals.shape[0]
    occ_local = kc_local // virt_count
    rows_pair = amplitudes.shape[0]
    cols_pair = integrals.shape[1]
    rows_device = rows_pair // contr_count
    slab_first = amplitudes.shape[0] * pair_count // occ_irrep.shape[0]
    slab_second = cols_pair * pair_count // occ_irrep.shape[0]
    first_start = slab_start[0]
    second_start = slab_start[1]
    a_irrep = lax.dynamic_slice(virt_irrep, (first_start,), (slab_first,))
    b_irrep = lax.dynamic_slice(virt_irrep, (second_start,), (slab_second,))
    a_energy = lax.dynamic_slice(virt_energy, (first_start,), (slab_first,))
    b_energy = lax.dynamic_slice(virt_energy, (second_start,), (slab_second,))
    row_irrep = jnp.bitwise_xor(occ_irrep[:, None], a_irrep[None, :]).reshape(-1)
    col_irrep = jnp.bitwise_xor(occ_irrep[:, None], b_irrep[None, :]).reshape(-1)
    row_energy = (occ_energy[:, None] - a_energy[None, :]).reshape(-1)
    col_energy = (occ_energy[:, None] - b_energy[None, :]).reshape(-1)
    whole_int = lax.all_gather(integrals, "pair", axis=1, tiled=True)
    partial = masked_product(slab_start, occ_irrep, virt_irrep, amplitudes, whole_int)
    if contr_count & (contr_count - 1) == 0 and rows_pair % contr_count == 0:
        summed = halving_scatter(partial, "contr", contr_count, contr_index)
    else:
        summed = lax.psum_scatter(partial, "contr", scatter_dimension=0, tiled=True)
    mine_irrep = lax.dynamic_slice(
        row_irrep, (pair_index * rows_pair + contr_index * rows_device,), (rows_device,)
    )
    summed = jnp.where(mine_irrep[:, None] == col_irrep[None, :], summed, 0.0)
    mine_energy = lax.dynamic_slice(
        row_energy, (pair_index * rows_pair + contr_index * rows_device,), (rows_device,)
    )
    update = (summed / (mine_energy[:, None] + col_energy[None, :])).astype(jnp.bfloat16)
    return update


def solution(mesh):
    in_specs = (P("pair", "contr"), P("contr", "pair"), P(), P(), P(), P(), P())
    out_specs = P(("pair", "contr"), None)
    return jax.shard_map(body, mesh=mesh, in_specs=in_specs, out_specs=out_specs, check_vma=False)
```

```python
import jax
import jax.numpy as jnp
from jax import lax
from jax.experimental import pallas as pl
from jax.experimental.pallas import tpu as pltpu
from jax.sharding import Mesh, PartitionSpec as P


def halving_scatter(partial, axes, count, index, tail):
    rows, cols = partial.shape
    block = rows // count
    bits = (count // tail).bit_length() - 1
    first = (index & 1) == 0

    def order(c):
        seq = list(range(bits))
        if c == 1 and bits >= 3:
            seq[1], seq[2] = seq[2], seq[1]
        return seq

    buf = partial.reshape((tail,) + (2,) * bits + (block, cols))
    left = [list(range(bits - 1, -1, -1)) for _ in range(2)]
    for stage in range(bits):
        split = [order(c)[stage] for c in range(2)]
        where = [1 + left[c].index(split[c]) for c in range(2)]
        mine = [(index >> split[c]) & 1 for c in range(2)]
        if where[0] == where[1]:
            bit = jnp.where(first, mine[0], mine[1]) if split[0] != split[1] else mine[0]
            keep = lax.dynamic_index_in_dim(buf, bit, axis=where[0], keepdims=False)
            send = lax.dynamic_index_in_dim(buf, 1 - bit, axis=where[0], keepdims=False)
        else:
            picks = [
                [lax.dynamic_index_in_dim(buf, v, axis=where[c], keepdims=False)
                 for v in (mine[c], 1 - mine[c])]
                for c in range(2)
            ]
            keep = jnp.where(first, picks[0][0], picks[1][0])
            send = jnp.where(first, picks[0][1], picks[1][1])
        for c in range(2):
            left[c].pop(where[c] - 1)
        perm = [(i, i ^ (1 << order(i & 1)[stage])) for i in range(count)]
        buf = keep + lax.ppermute(send, axes, perm)
    buf = buf.reshape(tail * block, cols)
    if tail > 1:
        got = lax.all_to_all(buf, axes[0], 0, 0, tiled=True)
        buf = got.reshape(tail, block, cols).sum(axis=0)
    return buf


def _masked_product_kernel(slab_ref, occ_s_ref, occ_v_ref, virt_v_ref, amp_ref, int_ref, out_ref):
    virt_count = virt_v_ref.shape[0]
    occ_count = occ_v_ref.shape[0]
    kc_local, cols = int_ref.shape
    occ_local = kc_local // virt_count
    per_occ = cols // occ_count
    second_start = slab_ref[1]
    base = (lax.axis_index("hi") * lax.axis_size("lo") + lax.axis_index("lo")) * occ_local
    f32, bf16 = jnp.float32, jnp.bfloat16
    occ_rows = jnp.broadcast_to(occ_v_ref[...].reshape(1, occ_count), (8, occ_count)).astype(bf16)
    virt_rows = jnp.broadcast_to(virt_v_ref[...].reshape(1, virt_count), (8, virt_count)).astype(bf16)
    q_of = lax.broadcasted_iota(jnp.int32, (occ_count, cols), 1)
    j_of = lax.broadcasted_iota(jnp.int32, (occ_count, cols), 0)
    occ_pick = (q_of // per_occ == j_of).astype(bf16)
    q_of = lax.broadcasted_iota(jnp.int32, (virt_count, cols), 1)
    c_of = lax.broadcasted_iota(jnp.int32, (virt_count, cols), 0)
    virt_pick = (c_of == second_start + q_of % per_occ).astype(bf16)
    col_occ = jnp.dot(occ_rows, occ_pick, preferred_element_type=f32)
    col_virt = jnp.dot(virt_rows, virt_pick, preferred_element_type=f32)
    col_irrep = jnp.bitwise_xor(col_occ.astype(jnp.int32), col_virt.astype(jnp.int32))[0:1, :]
    eye = (lax.broadcasted_iota(jnp.int32, (virt_count, virt_count), 0)
           == lax.broadcasted_iota(jnp.int32, (virt_count, virt_count), 1)).astype(bf16)
    virt_col = lax.dot_general(eye, virt_rows, (((1,), (1,)), ((), ())), preferred_element_type=f32)
    virt_col = virt_col.astype(jnp.int32)[:, 0:1]
    total = None
    for k in range(occ_local):
        kc_irrep = jnp.bitwise_xor(virt_col, occ_s_ref[base + k])
        block = int_ref[k * virt_count:(k + 1) * virt_count, :]
        masked = jnp.where(kc_irrep == col_irrep, block, jnp.zeros_like(block))
        term = jnp.dot(amp_ref[:, k * virt_count:(k + 1) * virt_count], masked, preferred_element_type=f32)
        total = term if total is None else total + term
    out_ref[...] = total


def masked_product(slab_start, occ_irrep, virt_irrep, amplitudes, integrals):
    rows, kc_local = amplitudes.shape
    cols = integrals.shape[1]
    smem = pl.BlockSpec(memory_space=pltpu.SMEM)
    vmem = pl.BlockSpec(memory_space=pltpu.VMEM)
    return pl.pallas_call(
        _masked_product_kernel,
        out_shape=jax.ShapeDtypeStruct((rows, cols), jnp.float32),
        in_specs=[smem, smem, vmem, vmem, vmem, vmem],
        out_specs=vmem,
        cost_estimate=pl.CostEstimate(
            flops=2 * rows * kc_local * cols,
            bytes_accessed=2 * rows * kc_local + 2 * kc_local * cols + 4 * rows * cols,
            transcendentals=0,
        ),
    )(slab_start, occ_irrep, occ_irrep, virt_irrep, amplitudes, integrals)


def body(amplitudes, integrals, occ_irrep, virt_irrep, occ_energy, virt_energy, slab_start):
    pair_count = lax.axis_size("pair")
    contr_count = lax.axis_size("hi") * lax.axis_size("lo")
    pair_index = lax.axis_index("pair")
    contr_index = lax.axis_index("hi") * lax.axis_size("lo") + lax.axis_index("lo")
    virt_count = virt_irrep.shape[0]
    kc_local = integrals.shape[0]
    occ_local = kc_local // virt_count
    rows_pair = amplitudes.shape[0]
    cols_pair = integrals.shape[1]
    rows_device = rows_pair // contr_count
    slab_first = amplitudes.shape[0] * pair_count // occ_irrep.shape[0]
    slab_second = cols_pair * pair_count // occ_irrep.shape[0]
    first_start = slab_start[0]
    second_start = slab_start[1]
    a_irrep = lax.dynamic_slice(virt_irrep, (first_start,), (slab_first,))
    b_irrep = lax.dynamic_slice(virt_irrep, (second_start,), (slab_second,))
    a_energy = lax.dynamic_slice(virt_energy, (first_start,), (slab_first,))
    b_energy = lax.dynamic_slice(virt_energy, (second_start,), (slab_second,))
    row_irrep = jnp.bitwise_xor(occ_irrep[:, None], a_irrep[None, :]).reshape(-1)
    col_irrep = jnp.bitwise_xor(occ_irrep[:, None], b_irrep[None, :]).reshape(-1)
    row_energy = (occ_energy[:, None] - a_energy[None, :]).reshape(-1)
    col_energy = (occ_energy[:, None] - b_energy[None, :]).reshape(-1)
    whole_int = lax.all_gather(integrals, "pair", axis=1, tiled=True)
    partial = masked_product(slab_start, occ_irrep, virt_irrep, amplitudes, whole_int)
    summed = halving_scatter(partial, ("hi", "lo"), contr_count, contr_index, lax.axis_size("hi"))
    mine_irrep = lax.dynamic_slice(
        row_irrep, (pair_index * rows_pair + contr_index * rows_device,), (rows_device,)
    )
    summed = jnp.where(mine_irrep[:, None] == col_irrep[None, :], summed, 0.0)
    mine_energy = lax.dynamic_slice(
        row_energy, (pair_index * rows_pair + contr_index * rows_device,), (rows_device,)
    )
    update = (summed / (mine_energy[:, None] + col_energy[None, :])).astype(jnp.bfloat16)
    return update


def solution(mesh):
    pair_count, contr_count = mesh.devices.shape
    lo = 8 if contr_count % 8 == 0 and contr_count & (contr_count - 1) == 0 else contr_count
    view = Mesh(mesh.devices.reshape(pair_count, contr_count // lo, lo), ("pair", "hi", "lo"))
    contr = ("hi", "lo")
    in_specs = (P("pair", contr), P(contr, "pair"), P(), P(), P(), P(), P())
    out_specs = P(("pair",) + contr, None)
    return jax.shard_map(body, mesh=view, in_specs=in_specs, out_specs=out_specs, check_vma=False)
```

```python
import functools

import jax
import jax.numpy as jnp
from jax import lax
from jax.experimental import pallas as pl
from jax.experimental.pallas import tpu as pltpu
from jax.sharding import PartitionSpec as P


def halving_scatter(partial, axis, count, index, second=None):
    rows, cols = partial.shape
    if second is not None:
        rows = 2 * rows
    block = rows // count
    bits = count.bit_length() - 1
    first = (index & 1) == 0

    def order(c):
        seq = list(range(bits))
        if c == 1 and bits >= 3:
            seq[1], seq[2] = seq[2], seq[1]
        return seq

    left = [list(range(bits - 1, -1, -1)) for _ in range(2)]
    stages = range(bits)
    if second is not None:
        got = lax.ppermute(partial, axis, [(i, i ^ 1) for i in range(count)])
        buf = (second() + got).reshape((2,) * (bits - 1) + (block, cols))
        left = [seq[:-1] for seq in left]
        stages = range(1, bits)
    else:
        buf = partial.reshape((2,) * bits + (block, cols))
    for stage in stages:
        split = [order(c)[stage] for c in range(2)]
        where = [left[c].index(split[c]) for c in range(2)]
        mine = [(index >> split[c]) & 1 for c in range(2)]
        if where[0] == where[1]:
            bit = jnp.where(first, mine[0], mine[1]) if split[0] != split[1] else mine[0]
            keep = lax.dynamic_index_in_dim(buf, bit, axis=where[0], keepdims=False)
            send = lax.dynamic_index_in_dim(buf, 1 - bit, axis=where[0], keepdims=False)
        else:
            picks = [
                [lax.dynamic_index_in_dim(buf, v, axis=where[c], keepdims=False)
                 for v in (mine[c], 1 - mine[c])]
                for c in range(2)
            ]
            keep = jnp.where(first, picks[0][0], picks[1][0])
            send = jnp.where(first, picks[0][1], picks[1][1])
        for c in range(2):
            left[c].pop(where[c])
        perm = [(i, i ^ (1 << order(i & 1)[stage])) for i in range(count)]
        buf = keep + lax.ppermute(send, axis, perm)
    return buf.reshape(block, cols)


def _irrep_mask(slab_ref, occ_s_ref, occ_v_ref, virt_v_ref, int_ref):
    virt_count = virt_v_ref.shape[0]
    occ_count = occ_v_ref.shape[0]
    kc_local, cols = int_ref.shape
    occ_local = kc_local // virt_count
    per_occ = cols // occ_count
    second_start = slab_ref[1]
    base = lax.axis_index("contr") * occ_local
    f32, bf16 = jnp.float32, jnp.bfloat16
    occ_rows = jnp.broadcast_to(occ_v_ref[...].reshape(1, occ_count), (8, occ_count)).astype(bf16)
    virt_rows = jnp.broadcast_to(virt_v_ref[...].reshape(1, virt_count), (8, virt_count)).astype(bf16)
    q_of = lax.broadcasted_iota(jnp.int32, (occ_count, cols), 1)
    j_of = lax.broadcasted_iota(jnp.int32, (occ_count, cols), 0)
    occ_pick = (q_of // per_occ == j_of).astype(bf16)
    q_of = lax.broadcasted_iota(jnp.int32, (virt_count, cols), 1)
    c_of = lax.broadcasted_iota(jnp.int32, (virt_count, cols), 0)
    virt_pick = (c_of == second_start + q_of % per_occ).astype(bf16)
    col_occ = jnp.dot(occ_rows, occ_pick, preferred_element_type=f32)
    col_virt = jnp.dot(virt_rows, virt_pick, preferred_element_type=f32)
    col_irrep = jnp.bitwise_xor(col_occ.astype(jnp.int32), col_virt.astype(jnp.int32))[0:1, :]
    eye = (lax.broadcasted_iota(jnp.int32, (virt_count, virt_count), 0)
           == lax.broadcasted_iota(jnp.int32, (virt_count, virt_count), 1)).astype(bf16)
    virt_col = lax.dot_general(eye, virt_rows, (((1,), (1,)), ((), ())), preferred_element_type=f32)
    virt_col = virt_col.astype(jnp.int32)[:, 0:1]
    parts = []
    for k in range(occ_local):
        kc_irrep = jnp.bitwise_xor(virt_col, occ_s_ref[base + k])
        block = int_ref[k * virt_count:(k + 1) * virt_count, :]
        parts.append(jnp.where(kc_irrep == col_irrep, block, jnp.zeros_like(block)))
    return parts


def _masked_product_kernel(slab_ref, occ_s_ref, occ_v_ref, virt_v_ref, amp_ref, int_ref, out_ref):
    virt_count = virt_v_ref.shape[0]
    total = None
    for k, masked in enumerate(_irrep_mask(slab_ref, occ_s_ref, occ_v_ref, virt_v_ref, int_ref)):
        term = jnp.dot(amp_ref[:, k * virt_count:(k + 1) * virt_count], masked,
                       preferred_element_type=jnp.float32)
        total = term if total is None else total + term
    out_ref[...] = total


def _half_rows(block, keep, amp_hbm, amp_buf, sems):
    core = lax.axis_index("contr") % 2
    parity = core if keep else 1 - core
    copies = []
    for m in range(amp_buf.shape[0] // block):
        src = amp_hbm.at[pl.ds(pl.multiple_of((2 * m + parity) * block, block), block), :]
        copy = pltpu.make_async_copy(src, amp_buf.at[pl.ds(m * block, block), :], sems.at[m])
        copy.start()
        copies.append(copy)
    return copies


def _send_half_kernel(block, slab_ref, occ_s_ref, occ_v_ref, virt_v_ref, amp_hbm, int_ref,
                      out_ref, masked_ref, amp_buf, sems):
    copies = _half_rows(block, False, amp_hbm, amp_buf, sems)
    parts = _irrep_mask(slab_ref, occ_s_ref, occ_v_ref, virt_v_ref, int_ref)
    virt_count = virt_v_ref.shape[0]
    for k, masked in enumerate(parts):
        masked_ref[k * virt_count:(k + 1) * virt_count, :] = masked
    for copy in copies:
        copy.wait()
    out_ref[...] = jnp.dot(amp_buf[...], masked_ref[...], preferred_element_type=jnp.float32)


def _keep_half_kernel(block, amp_hbm, masked_ref, out_ref, amp_buf, sems):
    copies = _half_rows(block, True, amp_hbm, amp_buf, sems)
    for copy in copies:
        copy.wait()
    out_ref[...] = jnp.dot(amp_buf[...], masked_ref[...], preferred_element_type=jnp.float32)


def masked_product(slab_start, occ_irrep, virt_irrep, amplitudes, integrals):
    rows, kc_local = amplitudes.shape
    cols = integrals.shape[1]
    smem = pl.BlockSpec(memory_space=pltpu.SMEM)
    vmem = pl.BlockSpec(memory_space=pltpu.VMEM)
    return pl.pallas_call(
        _masked_product_kernel,
        out_shape=jax.ShapeDtypeStruct((rows, cols), jnp.float32),
        in_specs=[smem, smem, vmem, vmem, vmem, vmem],
        out_specs=vmem,
        cost_estimate=pl.CostEstimate(
            flops=2 * rows * kc_local * cols,
            bytes_accessed=2 * rows * kc_local + 2 * kc_local * cols + 4 * rows * cols,
            transcendentals=0,
        ),
    )(slab_start, occ_irrep, occ_irrep, virt_irrep, amplitudes, integrals)


def split_product(block, slab_start, occ_irrep, virt_irrep, amplitudes, integrals):
    rows, kc_local = amplitudes.shape
    cols = integrals.shape[1]
    half = rows // 2
    smem = pl.BlockSpec(memory_space=pltpu.SMEM)
    vmem = pl.BlockSpec(memory_space=pltpu.VMEM)
    hbm = pl.BlockSpec(memory_space=pl.ANY)
    scratch = [pltpu.VMEM((half, kc_local), jnp.bfloat16), pltpu.SemaphoreType.DMA((half // block,))]
    cost = pl.CostEstimate(
        flops=2 * half * kc_local * cols,
        bytes_accessed=2 * half * kc_local + 2 * kc_local * cols + 4 * half * cols,
        transcendentals=0,
    )
    send, masked = pl.pallas_call(
        functools.partial(_send_half_kernel, block),
        out_shape=(jax.ShapeDtypeStruct((half, cols), jnp.float32),
                   jax.ShapeDtypeStruct((kc_local, cols), jnp.bfloat16)),
        in_specs=[smem, smem, vmem, vmem, hbm, vmem],
        out_specs=(vmem, vmem),
        scratch_shapes=scratch,
        cost_estimate=cost,
    )(slab_start, occ_irrep, occ_irrep, virt_irrep, amplitudes, integrals)
    keep_fn = pl.pallas_call(
        functools.partial(_keep_half_kernel, block),
        out_shape=jax.ShapeDtypeStruct((half, cols), jnp.float32),
        in_specs=[hbm, vmem],
        out_specs=vmem,
        scratch_shapes=scratch,
        cost_estimate=cost,
    )
    return send, lambda: keep_fn(amplitudes, masked)


def body(amplitudes, integrals, occ_irrep, virt_irrep, occ_energy, virt_energy, slab_start):
    pair_count = lax.axis_size("pair")
    contr_count = lax.axis_size("contr")
    pair_index = lax.axis_index("pair")
    contr_index = lax.axis_index("contr")
    virt_count = virt_irrep.shape[0]
    kc_local = integrals.shape[0]
    occ_local = kc_local // virt_count
    rows_pair = amplitudes.shape[0]
    cols_pair = integrals.shape[1]
    rows_device = rows_pair // contr_count
    slab_first = amplitudes.shape[0] * pair_count // occ_irrep.shape[0]
    slab_second = cols_pair * pair_count // occ_irrep.shape[0]
    first_start = slab_start[0]
    second_start = slab_start[1]
    a_irrep = lax.dynamic_slice(virt_irrep, (first_start,), (slab_first,))
    b_irrep = lax.dynamic_slice(virt_irrep, (second_start,), (slab_second,))
    a_energy = lax.dynamic_slice(virt_energy, (first_start,), (slab_first,))
    b_energy = lax.dynamic_slice(virt_energy, (second_start,), (slab_second,))
    row_irrep = jnp.bitwise_xor(occ_irrep[:, None], a_irrep[None, :]).reshape(-1)
    col_irrep = jnp.bitwise_xor(occ_irrep[:, None], b_irrep[None, :]).reshape(-1)
    row_energy = (occ_energy[:, None] - a_energy[None, :]).reshape(-1)
    col_energy = (occ_energy[:, None] - b_energy[None, :]).reshape(-1)
    whole_int = lax.all_gather(integrals, "pair", axis=1, tiled=True)
    power = contr_count & (contr_count - 1) == 0 and rows_pair % contr_count == 0
    block = rows_pair // contr_count
    if power and contr_count >= 2 and block % 16 == 0:
        send, keep = split_product(block, slab_start, occ_irrep, virt_irrep, amplitudes, whole_int)
        summed = halving_scatter(send, "contr", contr_count, contr_index, keep)
    else:
        partial = masked_product(slab_start, occ_irrep, virt_irrep, amplitudes, whole_int)
        if power:
            summed = halving_scatter(partial, "contr", contr_count, contr_index)
        else:
            summed = lax.psum_scatter(partial, "contr", scatter_dimension=0, tiled=True)
    mine_irrep = lax.dynamic_slice(
        row_irrep, (pair_index * rows_pair + contr_index * rows_device,), (rows_device,)
    )
    summed = jnp.where(mine_irrep[:, None] == col_irrep[None, :], summed, 0.0)
    mine_energy = lax.dynamic_slice(
        row_energy, (pair_index * rows_pair + contr_index * rows_device,), (rows_device,)
    )
    update = (summed / (mine_energy[:, None] + col_energy[None, :])).astype(jnp.bfloat16)
    return update


def solution(mesh):
    in_specs = (P("pair", "contr"), P("contr", "pair"), P(), P(), P(), P(), P())
    out_specs = P(("pair", "contr"), None)
    return jax.shard_map(body, mesh=mesh, in_specs=in_specs, out_specs=out_specs, check_vma=False)
```

```python
import jax
import jax.numpy as jnp
from jax import lax
from jax.experimental import pallas as pl
from jax.experimental.pallas import tpu as pltpu
from jax.sharding import PartitionSpec as P


def halving_scatter(partial, axis, count, index):
    rows, cols = partial.shape
    block = rows // count
    bits = count.bit_length() - 1
    first = (index & 1) == 0

    def order(c):
        seq = list(range(bits))
        if c == 1 and bits >= 3:
            seq[1], seq[2] = seq[2], seq[1]
        return seq

    buf = partial.reshape((2,) * bits + (block, cols))
    left = [list(range(bits - 1, -1, -1)) for _ in range(2)]
    for stage in range(bits):
        split = [order(c)[stage] for c in range(2)]
        where = [left[c].index(split[c]) for c in range(2)]
        mine = [(index >> split[c]) & 1 for c in range(2)]
        if where[0] == where[1]:
            bit = jnp.where(first, mine[0], mine[1]) if split[0] != split[1] else mine[0]
            keep = lax.dynamic_index_in_dim(buf, bit, axis=where[0], keepdims=False)
            send = lax.dynamic_index_in_dim(buf, 1 - bit, axis=where[0], keepdims=False)
        else:
            picks = [
                [lax.dynamic_index_in_dim(buf, v, axis=where[c], keepdims=False)
                 for v in (mine[c], 1 - mine[c])]
                for c in range(2)
            ]
            keep = jnp.where(first, picks[0][0], picks[1][0])
            send = jnp.where(first, picks[0][1], picks[1][1])
        for c in range(2):
            left[c].pop(where[c])
        perm = [(i, i ^ (1 << order(i & 1)[stage])) for i in range(count)]
        buf = keep + lax.ppermute(send, axis, perm)
    return buf.reshape(block, cols)


def _masked_product_kernel(slab_ref, occ_s_ref, occ_v_ref, virt_v_ref, amp_ref, int_ref, out_ref):
    virt_count = virt_v_ref.shape[0]
    occ_count = occ_v_ref.shape[0]
    kc_local, cols = int_ref.shape
    occ_local = kc_local // virt_count
    per_occ = cols // occ_count
    second_start = slab_ref[1]
    base = lax.axis_index("contr") * occ_local
    f32, bf16 = jnp.float32, jnp.bfloat16
    occ_rows = jnp.broadcast_to(occ_v_ref[...].reshape(1, occ_count), (8, occ_count)).astype(bf16)
    virt_rows = jnp.broadcast_to(virt_v_ref[...].reshape(1, virt_count), (8, virt_count)).astype(bf16)
    q_of = lax.broadcasted_iota(jnp.int32, (occ_count, cols), 1)
    j_of = lax.broadcasted_iota(jnp.int32, (occ_count, cols), 0)
    occ_pick = (q_of // per_occ == j_of).astype(bf16)
    q_of = lax.broadcasted_iota(jnp.int32, (virt_count, cols), 1)
    c_of = lax.broadcasted_iota(jnp.int32, (virt_count, cols), 0)
    virt_pick = (c_of == second_start + q_of % per_occ).astype(bf16)
    col_occ = jnp.dot(occ_rows, occ_pick, preferred_element_type=f32)
    col_virt = jnp.dot(virt_rows, virt_pick, preferred_element_type=f32)
    col_irrep = jnp.bitwise_xor(col_occ.astype(jnp.int32), col_virt.astype(jnp.int32))[0:1, :]
    eye = (lax.broadcasted_iota(jnp.int32, (virt_count, virt_count), 0)
           == lax.broadcasted_iota(jnp.int32, (virt_count, virt_count), 1)).astype(bf16)
    virt_col = lax.dot_general(eye, virt_rows, (((1,), (1,)), ((), ())), preferred_element_type=f32)
    virt_col = virt_col.astype(jnp.int32)[:, 0:1]
    total = None
    for k in range(occ_local):
        kc_irrep = jnp.bitwise_xor(virt_col, occ_s_ref[base + k])
        block = int_ref[k * virt_count:(k + 1) * virt_count, :]
        masked = jnp.where(kc_irrep == col_irrep, block, jnp.zeros_like(block))
        term = jnp.dot(amp_ref[:, k * virt_count:(k + 1) * virt_count], masked, preferred_element_type=f32)
        total = term if total is None else total + term
    out_ref[...] = total


def masked_product(slab_start, occ_irrep, virt_irrep, amplitudes, integrals):
    rows, kc_local = amplitudes.shape
    cols = integrals.shape[1]
    smem = pl.BlockSpec(memory_space=pltpu.SMEM)
    vmem = pl.BlockSpec(memory_space=pltpu.VMEM)
    return pl.pallas_call(
        _masked_product_kernel,
        out_shape=jax.ShapeDtypeStruct((rows, cols), jnp.float32),
        in_specs=[smem, smem, vmem, vmem, vmem, vmem],
        out_specs=vmem,
        compiler_params=pltpu.CompilerParams(vmem_limit_bytes=16 * 1024 * 1024),
        cost_estimate=pl.CostEstimate(
            flops=2 * rows * kc_local * cols,
            bytes_accessed=2 * rows * kc_local + 2 * kc_local * cols + 4 * rows * cols,
            transcendentals=0,
        ),
    )(slab_start, occ_irrep, occ_irrep, virt_irrep, amplitudes, integrals)


def body(amplitudes, integrals, occ_irrep, virt_irrep, occ_energy, virt_energy, slab_start):
    pair_count = lax.axis_size("pair")
    contr_count = lax.axis_size("contr")
    pair_index = lax.axis_index("pair")
    contr_index = lax.axis_index("contr")
    virt_count = virt_irrep.shape[0]
    kc_local = integrals.shape[0]
    occ_local = kc_local // virt_count
    rows_pair = amplitudes.shape[0]
    cols_pair = integrals.shape[1]
    rows_device = rows_pair // contr_count
    slab_first = amplitudes.shape[0] * pair_count // occ_irrep.shape[0]
    slab_second = cols_pair * pair_count // occ_irrep.shape[0]
    first_start = slab_start[0]
    second_start = slab_start[1]
    a_irrep = lax.dynamic_slice(virt_irrep, (first_start,), (slab_first,))
    b_irrep = lax.dynamic_slice(virt_irrep, (second_start,), (slab_second,))
    a_energy = lax.dynamic_slice(virt_energy, (first_start,), (slab_first,))
    b_energy = lax.dynamic_slice(virt_energy, (second_start,), (slab_second,))
    row_irrep = jnp.bitwise_xor(occ_irrep[:, None], a_irrep[None, :]).reshape(-1)
    col_irrep = jnp.bitwise_xor(occ_irrep[:, None], b_irrep[None, :]).reshape(-1)
    row_energy = (occ_energy[:, None] - a_energy[None, :]).reshape(-1)
    col_energy = (occ_energy[:, None] - b_energy[None, :]).reshape(-1)
    whole_int = lax.all_gather(integrals, "pair", axis=1, tiled=True)
    partial = masked_product(slab_start, occ_irrep, virt_irrep, amplitudes, whole_int)
    if contr_count & (contr_count - 1) == 0 and rows_pair % contr_count == 0:
        summed = halving_scatter(partial, "contr", contr_count, contr_index)
    else:
        summed = lax.psum_scatter(partial, "contr", scatter_dimension=0, tiled=True)
    mine_irrep = lax.dynamic_slice(
        row_irrep, (pair_index * rows_pair + contr_index * rows_device,), (rows_device,)
    )
    summed = jnp.where(mine_irrep[:, None] == col_irrep[None, :], summed, 0.0)
    mine_energy = lax.dynamic_slice(
        row_energy, (pair_index * rows_pair + contr_index * rows_device,), (rows_device,)
    )
    update = (summed / (mine_energy[:, None] + col_energy[None, :])).astype(jnp.bfloat16)
    return update


def solution(mesh):
    in_specs = (P("pair", "contr"), P("contr", "pair"), P(), P(), P(), P(), P())
    out_specs = P(("pair", "contr"), None)
    return jax.shard_map(body, mesh=mesh, in_specs=in_specs, out_specs=out_specs, check_vma=False)
```

```python
import jax
import jax.numpy as jnp
from jax import lax
from jax.experimental import pallas as pl
from jax.experimental.pallas import tpu as pltpu
from jax.sharding import PartitionSpec as P


def halving_scatter(partial, axis, count, index):
    rows, cols = partial.shape
    block = rows // count
    bits = count.bit_length() - 1
    first = (index & 1) == 0

    def order(c):
        seq = list(range(bits))
        if c == 1 and bits >= 3:
            seq[1], seq[2] = seq[2], seq[1]
        return seq

    buf = partial.reshape((2,) * bits + (block, cols))
    left = [list(range(bits - 1, -1, -1)) for _ in range(2)]
    for stage in range(bits):
        split = [order(c)[stage] for c in range(2)]
        where = [left[c].index(split[c]) for c in range(2)]
        mine = [(index >> split[c]) & 1 for c in range(2)]
        if where[0] == where[1]:
            bit = jnp.where(first, mine[0], mine[1]) if split[0] != split[1] else mine[0]
            keep = lax.dynamic_index_in_dim(buf, bit, axis=where[0], keepdims=False)
            send = lax.dynamic_index_in_dim(buf, 1 - bit, axis=where[0], keepdims=False)
        else:
            picks = [
                [lax.dynamic_index_in_dim(buf, v, axis=where[c], keepdims=False)
                 for v in (mine[c], 1 - mine[c])]
                for c in range(2)
            ]
            keep = jnp.where(first, picks[0][0], picks[1][0])
            send = jnp.where(first, picks[0][1], picks[1][1])
        for c in range(2):
            left[c].pop(where[c])
        perm = [(i, i ^ (1 << order(i & 1)[stage])) for i in range(count)]
        buf = keep + lax.ppermute(send, axis, perm)
    return buf.reshape(block, cols)


def _masked_product_kernel(slab_hbm, occ_hbm, virt_hbm, amp_hbm, int_hbm, out_hbm,
                           slab_ref, occ_s_ref, occ_v_ref, virt_v_ref, amp_v, int_v, out_v, sems, out_sems):
    rows = amp_v.shape[0]
    chunks = amp_v.shape[0] // 256 if amp_v.shape[0] % 256 == 0 else 1
    step = rows // chunks
    small = [
        pltpu.make_async_copy(slab_hbm, slab_ref, sems.at[0]),
        pltpu.make_async_copy(occ_hbm, occ_s_ref, sems.at[1]),
        pltpu.make_async_copy(occ_hbm, occ_v_ref, sems.at[2]),
        pltpu.make_async_copy(virt_hbm, virt_v_ref, sems.at[3]),
        pltpu.make_async_copy(int_hbm, int_v, sems.at[4]),
    ]
    for copy in small:
        copy.start()
    parts = []
    for m in range(chunks):
        copy = pltpu.make_async_copy(amp_hbm.at[pl.ds(m * step, step), :], amp_v.at[pl.ds(m * step, step), :],
                                     sems.at[5 + m])
        copy.start()
        parts.append(copy)
    for copy in small[:4]:
        copy.wait()
    virt_count = virt_v_ref.shape[0]
    occ_count = occ_v_ref.shape[0]
    kc_local, cols = int_v.shape
    occ_local = kc_local // virt_count
    per_occ = cols // occ_count
    second_start = slab_ref[1]
    base = lax.axis_index("contr") * occ_local
    f32, bf16 = jnp.float32, jnp.bfloat16
    occ_rows = jnp.broadcast_to(occ_v_ref[...].reshape(1, occ_count), (8, occ_count)).astype(bf16)
    virt_rows = jnp.broadcast_to(virt_v_ref[...].reshape(1, virt_count), (8, virt_count)).astype(bf16)
    q_of = lax.broadcasted_iota(jnp.int32, (occ_count, cols), 1)
    j_of = lax.broadcasted_iota(jnp.int32, (occ_count, cols), 0)
    occ_pick = (q_of // per_occ == j_of).astype(bf16)
    q_of = lax.broadcasted_iota(jnp.int32, (virt_count, cols), 1)
    c_of = lax.broadcasted_iota(jnp.int32, (virt_count, cols), 0)
    virt_pick = (c_of == second_start + q_of % per_occ).astype(bf16)
    col_occ = jnp.dot(occ_rows, occ_pick, preferred_element_type=f32)
    col_virt = jnp.dot(virt_rows, virt_pick, preferred_element_type=f32)
    col_irrep = jnp.bitwise_xor(col_occ.astype(jnp.int32), col_virt.astype(jnp.int32))[0:1, :]
    eye = (lax.broadcasted_iota(jnp.int32, (virt_count, virt_count), 0)
           == lax.broadcasted_iota(jnp.int32, (virt_count, virt_count), 1)).astype(bf16)
    virt_col = lax.dot_general(eye, virt_rows, (((1,), (1,)), ((), ())), preferred_element_type=f32)
    virt_col = virt_col.astype(jnp.int32)[:, 0:1]
    small[4].wait()
    masks = []
    for k in range(occ_local):
        kc_irrep = jnp.bitwise_xor(virt_col, occ_s_ref[base + k])
        block = int_v[k * virt_count:(k + 1) * virt_count, :]
        masks.append(jnp.where(kc_irrep == col_irrep, block, jnp.zeros_like(block)))
    outs = []
    for m in range(chunks):
        parts[m].wait()
        total = None
        for k in range(occ_local):
            term = jnp.dot(amp_v[m * step:(m + 1) * step, k * virt_count:(k + 1) * virt_count], masks[k],
                           preferred_element_type=f32)
            total = term if total is None else total + term
        out_v[m * step:(m + 1) * step, :] = total
        rows_out = pltpu.make_async_copy(out_v.at[pl.ds(m * step, step), :], out_hbm.at[pl.ds(m * step, step), :],
                                         out_sems.at[m])
        rows_out.start()
        outs.append(rows_out)
    for rows_out in outs:
        rows_out.wait()


def masked_product(slab_start, occ_irrep, virt_irrep, amplitudes, integrals):
    rows, kc_local = amplitudes.shape
    cols = integrals.shape[1]
    hbm = pl.BlockSpec(memory_space=pl.ANY)
    vmem = pl.BlockSpec(memory_space=pltpu.VMEM)
    chunks = rows // 256 if rows % 256 == 0 else 1
    return pl.pallas_call(
        _masked_product_kernel,
        out_shape=jax.ShapeDtypeStruct((rows, cols), jnp.float32),
        in_specs=[hbm] * 5,
        out_specs=hbm,
        scratch_shapes=[
            pltpu.SMEM(slab_start.shape, jnp.int32),
            pltpu.SMEM(occ_irrep.shape, jnp.int32),
            pltpu.VMEM(occ_irrep.shape, jnp.int32),
            pltpu.VMEM(virt_irrep.shape, jnp.int32),
            pltpu.VMEM(amplitudes.shape, amplitudes.dtype),
            pltpu.VMEM(integrals.shape, integrals.dtype),
            pltpu.VMEM((rows, cols), jnp.float32),
            pltpu.SemaphoreType.DMA((5 + chunks,)),
            pltpu.SemaphoreType.DMA((chunks,)),
        ],
        cost_estimate=pl.CostEstimate(
            flops=2 * rows * kc_local * cols,
            bytes_accessed=2 * rows * kc_local + 2 * kc_local * cols + 4 * rows * cols,
            transcendentals=0,
        ),
    )(slab_start, occ_irrep, virt_irrep, amplitudes, integrals)


def body(amplitudes, integrals, occ_irrep, virt_irrep, occ_energy, virt_energy, slab_start):
    pair_count = lax.axis_size("pair")
    contr_count = lax.axis_size("contr")
    pair_index = lax.axis_index("pair")
    contr_index = lax.axis_index("contr")
    virt_count = virt_irrep.shape[0]
    kc_local = integrals.shape[0]
    occ_local = kc_local // virt_count
    rows_pair = amplitudes.shape[0]
    cols_pair = integrals.shape[1]
    rows_device = rows_pair // contr_count
    slab_first = amplitudes.shape[0] * pair_count // occ_irrep.shape[0]
    slab_second = cols_pair * pair_count // occ_irrep.shape[0]
    first_start = slab_start[0]
    second_start = slab_start[1]
    a_irrep = lax.dynamic_slice(virt_irrep, (first_start,), (slab_first,))
    b_irrep = lax.dynamic_slice(virt_irrep, (second_start,), (slab_second,))
    a_energy = lax.dynamic_slice(virt_energy, (first_start,), (slab_first,))
    b_energy = lax.dynamic_slice(virt_energy, (second_start,), (slab_second,))
    row_irrep = jnp.bitwise_xor(occ_irrep[:, None], a_irrep[None, :]).reshape(-1)
    col_irrep = jnp.bitwise_xor(occ_irrep[:, None], b_irrep[None, :]).reshape(-1)
    row_energy = (occ_energy[:, None] - a_energy[None, :]).reshape(-1)
    col_energy = (occ_energy[:, None] - b_energy[None, :]).reshape(-1)
    whole_int = lax.all_gather(integrals, "pair", axis=1, tiled=True)
    partial = masked_product(slab_start, occ_irrep, virt_irrep, amplitudes, whole_int)
    if contr_count & (contr_count - 1) == 0 and rows_pair % contr_count == 0:
        summed = halving_scatter(partial, "contr", contr_count, contr_index)
    else:
        summed = lax.psum_scatter(partial, "contr", scatter_dimension=0, tiled=True)
    mine_irrep = lax.dynamic_slice(
        row_irrep, (pair_index * rows_pair + contr_index * rows_device,), (rows_device,)
    )
    summed = jnp.where(mine_irrep[:, None] == col_irrep[None, :], summed, 0.0)
    mine_energy = lax.dynamic_slice(
        row_energy, (pair_index * rows_pair + contr_index * rows_device,), (rows_device,)
    )
    update = (summed / (mine_energy[:, None] + col_energy[None, :])).astype(jnp.bfloat16)
    return update


def solution(mesh):
    in_specs = (P("pair", "contr"), P("contr", "pair"), P(), P(), P(), P(), P())
    out_specs = P(("pair", "contr"), None)
    return jax.shard_map(body, mesh=mesh, in_specs=in_specs, out_specs=out_specs, check_vma=False)
```

```python
import functools

import jax
import jax.numpy as jnp
from jax import lax
from jax.experimental import pallas as pl
from jax.experimental.pallas import tpu as pltpu
from jax.sharding import PartitionSpec as P


def halving_scatter(partial, axis, count, index):
    rows, cols = partial.shape
    block = rows // count
    bits = count.bit_length() - 1
    first = (index & 1) == 0

    def order(c):
        seq = list(range(bits))
        if c == 1 and bits >= 3:
            seq[1], seq[2] = seq[2], seq[1]
        return seq

    buf = partial.reshape((2,) * bits + (block, cols))
    left = [list(range(bits - 1, -1, -1)) for _ in range(2)]
    for stage in range(bits):
        split = [order(c)[stage] for c in range(2)]
        where = [left[c].index(split[c]) for c in range(2)]
        mine = [(index >> split[c]) & 1 for c in range(2)]
        if where[0] == where[1]:
            bit = jnp.where(first, mine[0], mine[1]) if split[0] != split[1] else mine[0]
            keep = lax.dynamic_index_in_dim(buf, bit, axis=where[0], keepdims=False)
            send = lax.dynamic_index_in_dim(buf, 1 - bit, axis=where[0], keepdims=False)
        else:
            picks = [
                [lax.dynamic_index_in_dim(buf, v, axis=where[c], keepdims=False)
                 for v in (mine[c], 1 - mine[c])]
                for c in range(2)
            ]
            keep = jnp.where(first, picks[0][0], picks[1][0])
            send = jnp.where(first, picks[0][1], picks[1][1])
        for c in range(2):
            left[c].pop(where[c])
        perm = [(i, i ^ (1 << order(i & 1)[stage])) for i in range(count)]
        buf = keep + lax.ppermute(send, axis, perm)
    return buf.reshape(block, cols)


def _irrep_kernel(pair_rows, slab_ref, occ_s_ref, occ_v_ref, virt_v_ref, row_ref, kc_ref, col_ref):
    virt_count = virt_v_ref.shape[0]
    occ_count = occ_v_ref.shape[0]
    rows = row_ref.shape[1]
    kc_local = kc_ref.shape[1]
    cols = col_ref.shape[1]
    occ_local = kc_local // virt_count
    f32, bf16, i32 = jnp.float32, jnp.bfloat16, jnp.int32
    occ_rows = jnp.broadcast_to(occ_v_ref[...].reshape(1, occ_count), (8, occ_count)).astype(bf16)
    virt_rows = jnp.broadcast_to(virt_v_ref[...].reshape(1, virt_count), (8, virt_count)).astype(bf16)

    def spread(count, starts, per, dst):
        x_of = lax.broadcasted_iota(i32, (occ_count, count), 1)
        j_of = lax.broadcasted_iota(i32, (occ_count, count), 0)
        occ_part = jnp.dot(occ_rows, (x_of // per == j_of).astype(bf16), preferred_element_type=f32)
        x_of = lax.broadcasted_iota(i32, (virt_count, count), 1)
        c_of = lax.broadcasted_iota(i32, (virt_count, count), 0)
        virt_part = jnp.dot(virt_rows, (c_of == starts + x_of % per).astype(bf16), preferred_element_type=f32)
        return jnp.bitwise_xor(occ_part.astype(i32), virt_part.astype(i32))[0:1, :]

    per_row = rows * pair_rows // occ_count
    row_ref[...] = spread(rows, slab_ref[0], per_row, None)
    col_ref[...] = spread(cols, slab_ref[1], cols // occ_count, None)
    base = lax.axis_index("contr") * occ_local
    parts = [jnp.bitwise_xor(virt_v_ref[...].reshape(1, virt_count), occ_s_ref[base + k]) for k in range(occ_local)]
    kc_ref[...] = jnp.concatenate(parts, axis=1) if occ_local > 1 else parts[0]


def irreps(pair_count, slab_start, occ_irrep, virt_irrep, rows, kc_local, cols):
    smem = pl.BlockSpec(memory_space=pltpu.SMEM)
    vmem = pl.BlockSpec(memory_space=pltpu.VMEM)
    shapes = [jax.ShapeDtypeStruct((1, n), jnp.int32) for n in (rows, kc_local, cols)]
    return pl.pallas_call(
        functools.partial(_irrep_kernel, pair_count),
        out_shape=shapes,
        in_specs=[smem, smem, vmem, vmem],
        out_specs=[vmem, vmem, vmem],
    )(slab_start, occ_irrep, occ_irrep, virt_irrep)


def body(amplitudes, integrals, occ_irrep, virt_irrep, occ_energy, virt_energy, slab_start):
    pair_count = lax.axis_size("pair")
    contr_count = lax.axis_size("contr")
    pair_index = lax.axis_index("pair")
    contr_index = lax.axis_index("contr")
    virt_count = virt_irrep.shape[0]
    kc_local = integrals.shape[0]
    occ_local = kc_local // virt_count
    rows_pair = amplitudes.shape[0]
    cols_pair = integrals.shape[1]
    rows_device = rows_pair // contr_count
    slab_first = amplitudes.shape[0] * pair_count // occ_irrep.shape[0]
    slab_second = cols_pair * pair_count // occ_irrep.shape[0]
    first_start = slab_start[0]
    second_start = slab_start[1]
    a_irrep = lax.dynamic_slice(virt_irrep, (first_start,), (slab_first,))
    b_irrep = lax.dynamic_slice(virt_irrep, (second_start,), (slab_second,))
    a_energy = lax.dynamic_slice(virt_energy, (first_start,), (slab_first,))
    b_energy = lax.dynamic_slice(virt_energy, (second_start,), (slab_second,))
    row_irrep = jnp.bitwise_xor(occ_irrep[:, None], a_irrep[None, :]).reshape(-1)
    col_irrep = jnp.bitwise_xor(occ_irrep[:, None], b_irrep[None, :]).reshape(-1)
    row_energy = (occ_energy[:, None] - a_energy[None, :]).reshape(-1)
    col_energy = (occ_energy[:, None] - b_energy[None, :]).reshape(-1)
    zero = jnp.zeros((), jnp.bfloat16)
    whole_int = lax.all_gather(integrals, "pair", axis=1, tiled=True)
    row_k, kc_k, col_k = irreps(pair_count, slab_start, occ_irrep, virt_irrep,
                                rows_pair * pair_count, kc_local, cols_pair * pair_count)
    kc_irrep = kc_k.reshape(-1)
    int_masked = jnp.where(kc_irrep[:, None] == col_k.reshape(-1)[None, :], whole_int, zero)
    row_irrep_pair = lax.dynamic_slice(row_k.reshape(-1), (pair_index * rows_pair,), (rows_pair,))
    amp_masked = jnp.where(row_irrep_pair[:, None] == kc_irrep[None, :], amplitudes, zero)
    partial = jnp.dot(amp_masked, int_masked, preferred_element_type=jnp.float32)
    if contr_count & (contr_count - 1) == 0 and rows_pair % contr_count == 0:
        summed = halving_scatter(partial, "contr", contr_count, contr_index)
    else:
        summed = lax.psum_scatter(partial, "contr", scatter_dimension=0, tiled=True)
    mine_energy = lax.dynamic_slice(
        row_energy, (pair_index * rows_pair + contr_index * rows_device,), (rows_device,)
    )
    update = (summed / (mine_energy[:, None] + col_energy[None, :])).astype(jnp.bfloat16)
    return update


def solution(mesh):
    in_specs = (P("pair", "contr"), P("contr", "pair"), P(), P(), P(), P(), P())
    out_specs = P(("pair", "contr"), None)
    return jax.shard_map(body, mesh=mesh, in_specs=in_specs, out_specs=out_specs, check_vma=False)
```

```python
import functools

import jax
import jax.numpy as jnp
from jax import lax
from jax.experimental import pallas as pl
from jax.experimental.pallas import tpu as pltpu
from jax.sharding import PartitionSpec as P


def halving_scatter(partial, axis, count, index):
    rows, cols = partial.shape
    block = rows // count
    bits = count.bit_length() - 1
    first = (index & 1) == 0

    def order(c):
        seq = list(range(bits))
        if c == 1 and bits >= 3:
            seq[1], seq[2] = seq[2], seq[1]
        return seq

    buf = partial.reshape((2,) * bits + (block, cols))
    left = [list(range(bits - 1, -1, -1)) for _ in range(2)]
    for stage in range(bits):
        split = [order(c)[stage] for c in range(2)]
        where = [left[c].index(split[c]) for c in range(2)]
        mine = [(index >> split[c]) & 1 for c in range(2)]
        if where[0] == where[1]:
            bit = jnp.where(first, mine[0], mine[1]) if split[0] != split[1] else mine[0]
            keep = lax.dynamic_index_in_dim(buf, bit, axis=where[0], keepdims=False)
            send = lax.dynamic_index_in_dim(buf, 1 - bit, axis=where[0], keepdims=False)
        else:
            picks = [
                [lax.dynamic_index_in_dim(buf, v, axis=where[c], keepdims=False)
                 for v in (mine[c], 1 - mine[c])]
                for c in range(2)
            ]
            keep = jnp.where(first, picks[0][0], picks[1][0])
            send = jnp.where(first, picks[0][1], picks[1][1])
        for c in range(2):
            left[c].pop(where[c])
        perm = [(i, i ^ (1 << order(i & 1)[stage])) for i in range(count)]
        buf = keep + lax.ppermute(send, axis, perm)
    return buf.reshape(block, cols)


def _irrep_kernel(pair_rows, slab_ref, occ_s_ref, occ_v_ref, virt_v_ref, occ_e_ref, virt_e_ref,
                  row_ref, kc_ref, col_ref, denom_ref):
    virt_count = virt_v_ref.shape[0]
    occ_count = occ_v_ref.shape[0]
    rows = row_ref.shape[1]
    kc_local = kc_ref.shape[1]
    cols = col_ref.shape[1]
    occ_local = kc_local // virt_count
    f32, bf16, i32 = jnp.float32, jnp.bfloat16, jnp.int32
    occ_rows = jnp.broadcast_to(occ_v_ref[...].reshape(1, occ_count), (8, occ_count)).astype(bf16)
    virt_rows = jnp.broadcast_to(virt_v_ref[...].reshape(1, virt_count), (8, virt_count)).astype(bf16)

    def spread(count, starts, per, dst):
        x_of = lax.broadcasted_iota(i32, (occ_count, count), 1)
        j_of = lax.broadcasted_iota(i32, (occ_count, count), 0)
        occ_part = jnp.dot(occ_rows, (x_of // per == j_of).astype(bf16), preferred_element_type=f32)
        x_of = lax.broadcasted_iota(i32, (virt_count, count), 1)
        c_of = lax.broadcasted_iota(i32, (virt_count, count), 0)
        virt_part = jnp.dot(virt_rows, (c_of == starts + x_of % per).astype(bf16), preferred_element_type=f32)
        return jnp.bitwise_xor(occ_part.astype(i32), virt_part.astype(i32))[0:1, :]

    per_row = rows // occ_count
    row_ref[...] = spread(rows, slab_ref[0], per_row, None)
    col_ref[...] = spread(cols, slab_ref[1], cols // occ_count, None)
    base = lax.axis_index("contr") * occ_local
    parts = [jnp.bitwise_xor(virt_v_ref[...].reshape(1, virt_count), occ_s_ref[base + k]) for k in range(occ_local)]
    kc_ref[...] = jnp.concatenate(parts, axis=1) if occ_local > 1 else parts[0]
    mine, all_cols = denom_ref.shape
    per_col = all_cols // occ_count
    q_of = lax.broadcasted_iota(i32, (1, all_cols), 1)

    def col_step(j, acc):
        return jnp.where(q_of // per_col == j, occ_e_ref[j], acc)

    col_occ = lax.fori_loop(0, occ_count, col_step, jnp.zeros((1, all_cols), f32))
    col_virt = jnp.zeros((1, all_cols), f32)
    for b in range(per_col):
        col_virt = jnp.where(q_of % per_col == b, virt_e_ref[slab_ref[1] + b], col_virt)
    first_row = (lax.axis_index("pair") * lax.axis_size("contr") + lax.axis_index("contr")) * mine
    t_of = lax.broadcasted_iota(i32, (mine, all_cols), 0)
    row_occ = jnp.zeros((mine, all_cols), f32)
    row_virt = jnp.zeros((mine, all_cols), f32)
    for t in range(mine):
        r = first_row + t
        row_occ = jnp.where(t_of == t, occ_e_ref[r // per_row], row_occ)
        row_virt = jnp.where(t_of == t, virt_e_ref[slab_ref[0] + r % per_row], row_virt)
    denom_ref[...] = (row_occ - row_virt) + (col_occ - col_virt)


def irreps(pair_count, slab_start, occ_irrep, virt_irrep, occ_energy, virt_energy, rows, kc_local, cols, mine):
    smem = pl.BlockSpec(memory_space=pltpu.SMEM)
    vmem = pl.BlockSpec(memory_space=pltpu.VMEM)
    shapes = [jax.ShapeDtypeStruct((1, n), jnp.int32) for n in (rows, kc_local, cols)]
    shapes.append(jax.ShapeDtypeStruct((mine, cols), jnp.float32))
    return pl.pallas_call(
        functools.partial(_irrep_kernel, pair_count),
        out_shape=shapes,
        in_specs=[smem, smem, vmem, vmem, smem, smem],
        out_specs=[vmem, vmem, vmem, vmem],
    )(slab_start, occ_irrep, occ_irrep, virt_irrep, occ_energy, virt_energy)


def body(amplitudes, integrals, occ_irrep, virt_irrep, occ_energy, virt_energy, slab_start):
    pair_count = lax.axis_size("pair")
    contr_count = lax.axis_size("contr")
    pair_index = lax.axis_index("pair")
    contr_index = lax.axis_index("contr")
    virt_count = virt_irrep.shape[0]
    kc_local = integrals.shape[0]
    occ_local = kc_local // virt_count
    rows_pair = amplitudes.shape[0]
    cols_pair = integrals.shape[1]
    rows_device = rows_pair // contr_count
    zero = jnp.zeros((), jnp.bfloat16)
    whole_int = lax.all_gather(integrals, "pair", axis=1, tiled=True)
    row_k, kc_k, col_k, denom = irreps(pair_count, slab_start, occ_irrep, virt_irrep, occ_energy, virt_energy,
                                       rows_pair * pair_count, kc_local, cols_pair * pair_count, rows_device)
    kc_irrep = kc_k.reshape(-1)
    int_masked = jnp.where(kc_irrep[:, None] == col_k.reshape(-1)[None, :], whole_int, zero)
    row_irrep_pair = lax.dynamic_slice(row_k.reshape(-1), (pair_index * rows_pair,), (rows_pair,))
    amp_masked = jnp.where(row_irrep_pair[:, None] == kc_irrep[None, :], amplitudes, zero)
    partial = jnp.dot(amp_masked, int_masked, preferred_element_type=jnp.float32)
    if contr_count & (contr_count - 1) == 0 and rows_pair % contr_count == 0:
        summed = halving_scatter(partial, "contr", contr_count, contr_index)
    else:
        summed = lax.psum_scatter(partial, "contr", scatter_dimension=0, tiled=True)
    update = (summed / denom).astype(jnp.bfloat16)
    return update


def solution(mesh):
    in_specs = (P("pair", "contr"), P("contr", "pair"), P(), P(), P(), P(), P())
    out_specs = P(("pair", "contr"), None)
    return jax.shard_map(body, mesh=mesh, in_specs=in_specs, out_specs=out_specs, check_vma=False)
```

```python
import functools

import jax
import jax.numpy as jnp
from jax import lax
from jax.experimental import pallas as pl
from jax.experimental.pallas import tpu as pltpu
from jax.sharding import PartitionSpec as P


def halving_scatter(partial, axis, count, index, second=None):
    rows, cols = partial.shape
    if second is not None:
        rows = 2 * rows
    block = rows // count
    bits = count.bit_length() - 1
    first = (index & 1) == 0

    def order(c):
        seq = list(range(bits))
        if c == 1 and bits >= 3:
            seq[1], seq[2] = seq[2], seq[1]
        return seq

    left = [list(range(bits - 1, -1, -1)) for _ in range(2)]
    stages = range(bits)
    if second is not None:
        got = lax.ppermute(partial, axis, [(i, i ^ 1) for i in range(count)])
        buf = (second() + got).reshape((2,) * (bits - 1) + (block, cols))
        left = [seq[:-1] for seq in left]
        stages = range(1, bits)
    else:
        buf = partial.reshape((2,) * bits + (block, cols))
    for stage in stages:
        split = [order(c)[stage] for c in range(2)]
        where = [left[c].index(split[c]) for c in range(2)]
        mine = [(index >> split[c]) & 1 for c in range(2)]
        if where[0] == where[1]:
            bit = jnp.where(first, mine[0], mine[1]) if split[0] != split[1] else mine[0]
            keep = lax.dynamic_index_in_dim(buf, bit, axis=where[0], keepdims=False)
            send = lax.dynamic_index_in_dim(buf, 1 - bit, axis=where[0], keepdims=False)
        else:
            picks = [
                [lax.dynamic_index_in_dim(buf, v, axis=where[c], keepdims=False)
                 for v in (mine[c], 1 - mine[c])]
                for c in range(2)
            ]
            keep = jnp.where(first, picks[0][0], picks[1][0])
            send = jnp.where(first, picks[0][1], picks[1][1])
        for c in range(2):
            left[c].pop(where[c])
        perm = [(i, i ^ (1 << order(i & 1)[stage])) for i in range(count)]
        buf = keep + lax.ppermute(send, axis, perm)
    return buf.reshape(block, cols)


def _irrep_kernel(pair_rows, slab_ref, occ_s_ref, occ_v_ref, virt_v_ref, row_ref, kc_ref, col_ref):
    virt_count = virt_v_ref.shape[0]
    occ_count = occ_v_ref.shape[0]
    rows = row_ref.shape[1]
    kc_local = kc_ref.shape[1]
    cols = col_ref.shape[1]
    occ_local = kc_local // virt_count
    f32, bf16, i32 = jnp.float32, jnp.bfloat16, jnp.int32
    occ_rows = jnp.broadcast_to(occ_v_ref[...].reshape(1, occ_count), (8, occ_count)).astype(bf16)
    virt_rows = jnp.broadcast_to(virt_v_ref[...].reshape(1, virt_count), (8, virt_count)).astype(bf16)

    def spread(count, starts, per, dst):
        x_of = lax.broadcasted_iota(i32, (occ_count, count), 1)
        j_of = lax.broadcasted_iota(i32, (occ_count, count), 0)
        occ_part = jnp.dot(occ_rows, (x_of // per == j_of).astype(bf16), preferred_element_type=f32)
        x_of = lax.broadcasted_iota(i32, (virt_count, count), 1)
        c_of = lax.broadcasted_iota(i32, (virt_count, count), 0)
        virt_part = jnp.dot(virt_rows, (c_of == starts + x_of % per).astype(bf16), preferred_element_type=f32)
        return jnp.bitwise_xor(occ_part.astype(i32), virt_part.astype(i32))[0:1, :]

    per_row = rows // occ_count
    row_ref[...] = spread(rows, slab_ref[0], per_row, None)
    col_ref[...] = spread(cols, slab_ref[1], cols // occ_count, None)
    base = lax.axis_index("contr") * occ_local
    parts = [jnp.bitwise_xor(virt_v_ref[...].reshape(1, virt_count), occ_s_ref[base + k]) for k in range(occ_local)]
    kc_ref[...] = jnp.concatenate(parts, axis=1) if occ_local > 1 else parts[0]


def irreps(pair_count, slab_start, occ_irrep, virt_irrep, rows, kc_local, cols):
    smem = pl.BlockSpec(memory_space=pltpu.SMEM)
    vmem = pl.BlockSpec(memory_space=pltpu.VMEM)
    shapes = [jax.ShapeDtypeStruct((1, n), jnp.int32) for n in (rows, kc_local, cols)]
    return pl.pallas_call(
        functools.partial(_irrep_kernel, pair_count),
        out_shape=shapes,
        in_specs=[smem, smem, vmem, vmem],
        out_specs=[vmem, vmem, vmem],
    )(slab_start, occ_irrep, occ_irrep, virt_irrep)


def body(amplitudes, integrals, occ_irrep, virt_irrep, occ_energy, virt_energy, slab_start):
    pair_count = lax.axis_size("pair")
    contr_count = lax.axis_size("contr")
    pair_index = lax.axis_index("pair")
    contr_index = lax.axis_index("contr")
    virt_count = virt_irrep.shape[0]
    kc_local = integrals.shape[0]
    occ_local = kc_local // virt_count
    rows_pair = amplitudes.shape[0]
    cols_pair = integrals.shape[1]
    rows_device = rows_pair // contr_count
    slab_first = amplitudes.shape[0] * pair_count // occ_irrep.shape[0]
    slab_second = cols_pair * pair_count // occ_irrep.shape[0]
    first_start = slab_start[0]
    second_start = slab_start[1]
    a_irrep = lax.dynamic_slice(virt_irrep, (first_start,), (slab_first,))
    b_irrep = lax.dynamic_slice(virt_irrep, (second_start,), (slab_second,))
    a_energy = lax.dynamic_slice(virt_energy, (first_start,), (slab_first,))
    b_energy = lax.dynamic_slice(virt_energy, (second_start,), (slab_second,))
    row_irrep = jnp.bitwise_xor(occ_irrep[:, None], a_irrep[None, :]).reshape(-1)
    col_irrep = jnp.bitwise_xor(occ_irrep[:, None], b_irrep[None, :]).reshape(-1)
    row_energy = (occ_energy[:, None] - a_energy[None, :]).reshape(-1)
    col_energy = (occ_energy[:, None] - b_energy[None, :]).reshape(-1)
    zero = jnp.zeros((), jnp.bfloat16)
    whole_int = lax.all_gather(integrals, "pair", axis=1, tiled=True)
    row_k, kc_k, col_k = irreps(pair_count, slab_start, occ_irrep, virt_irrep,
                                rows_pair * pair_count, kc_local, cols_pair * pair_count)
    kc_irrep = kc_k.reshape(-1)
    int_masked = jnp.where(kc_irrep[:, None] == col_k.reshape(-1)[None, :], whole_int, zero)
    row_irrep_pair = lax.dynamic_slice(row_k.reshape(-1), (pair_index * rows_pair,), (rows_pair,))
    def product(amp, irrep):
        masked = jnp.where(irrep[:, None] == kc_irrep[None, :], amp, zero)
        return jnp.dot(masked, int_masked, preferred_element_type=jnp.float32)

    block = rows_pair // contr_count
    if contr_count & (contr_count - 1) == 0 and rows_pair % contr_count == 0 and contr_count >= 2:
        amp4 = amplitudes.reshape(rows_pair // (2 * block), 2, block, kc_local)
        irrep4 = row_irrep_pair.reshape(rows_pair // (2 * block), 2, block)
        core = contr_index % 2

        def half(parity):
            amp = lax.dynamic_index_in_dim(amp4, parity, axis=1, keepdims=False)
            irrep = lax.dynamic_index_in_dim(irrep4, parity, axis=1, keepdims=False)
            return product(amp.reshape(rows_pair // 2, kc_local), irrep.reshape(-1))

        summed = halving_scatter(half(1 - core), "contr", contr_count, contr_index,
                                 lambda: lax.optimization_barrier(half(core)))
    else:
        partial = product(amplitudes, row_irrep_pair)
        summed = lax.psum_scatter(partial, "contr", scatter_dimension=0, tiled=True)
    mine_energy = lax.dynamic_slice(
        row_energy, (pair_index * rows_pair + contr_index * rows_device,), (rows_device,)
    )
    update = (summed / (mine_energy[:, None] + col_energy[None, :])).astype(jnp.bfloat16)
    return update


def solution(mesh):
    in_specs = (P("pair", "contr"), P("contr", "pair"), P(), P(), P(), P(), P())
    out_specs = P(("pair", "contr"), None)
    return jax.shard_map(body, mesh=mesh, in_specs=in_specs, out_specs=out_specs, check_vma=False)
```

```python
import functools

import jax
import jax.numpy as jnp
from jax import lax
from jax.experimental import pallas as pl
from jax.experimental.pallas import tpu as pltpu
from jax.sharding import PartitionSpec as P


def halving_scatter(partial, axis, count, index, second=None):
    rows, cols = partial.shape
    if second is not None:
        rows = 2 * rows
    block = rows // count
    bits = count.bit_length() - 1
    first = (index & 1) == 0

    def order(c):
        seq = list(range(bits))
        if c == 1 and bits >= 3:
            seq[1], seq[2] = seq[2], seq[1]
        return seq

    left = [list(range(bits - 1, -1, -1)) for _ in range(2)]
    stages = range(bits)
    if second is not None:
        got = lax.ppermute(partial, axis, [(i, i ^ 1) for i in range(count)])
        buf = (second() + got).reshape((2,) * (bits - 1) + (block, cols))
        left = [seq[:-1] for seq in left]
        stages = range(1, bits)
    else:
        buf = partial.reshape((2,) * bits + (block, cols))
    for stage in stages:
        split = [order(c)[stage] for c in range(2)]
        where = [left[c].index(split[c]) for c in range(2)]
        mine = [(index >> split[c]) & 1 for c in range(2)]
        if where[0] == where[1]:
            bit = jnp.where(first, mine[0], mine[1]) if split[0] != split[1] else mine[0]
            keep = lax.dynamic_index_in_dim(buf, bit, axis=where[0], keepdims=False)
            send = lax.dynamic_index_in_dim(buf, 1 - bit, axis=where[0], keepdims=False)
        else:
            picks = [
                [lax.dynamic_index_in_dim(buf, v, axis=where[c], keepdims=False)
                 for v in (mine[c], 1 - mine[c])]
                for c in range(2)
            ]
            keep = jnp.where(first, picks[0][0], picks[1][0])
            send = jnp.where(first, picks[0][1], picks[1][1])
        for c in range(2):
            left[c].pop(where[c])
        perm = [(i, i ^ (1 << order(i & 1)[stage])) for i in range(count)]
        buf = keep + lax.ppermute(send, axis, perm)
    return buf.reshape(block, cols)


def _irrep_kernel(shape, slab_ref, occ_s_ref, occ_v_ref, virt_v_ref, row_ref, kc_ref, col_ref):
    virt_count = virt_v_ref.shape[0]
    occ_count = occ_v_ref.shape[0]
    kc_local = kc_ref.shape[1]
    cols = col_ref.shape[1]
    occ_local = kc_local // virt_count
    f32, bf16, i32 = jnp.float32, jnp.bfloat16, jnp.int32
    occ_rows = jnp.broadcast_to(occ_v_ref[...].reshape(1, occ_count), (8, occ_count)).astype(bf16)
    virt_rows = jnp.broadcast_to(virt_v_ref[...].reshape(1, virt_count), (8, virt_count)).astype(bf16)

    def spread(count, starts, per, where=lambda x: x):
        x_of = where(lax.broadcasted_iota(i32, (occ_count, count), 1))
        j_of = lax.broadcasted_iota(i32, (occ_count, count), 0)
        occ_part = jnp.dot(occ_rows, (x_of // per == j_of).astype(bf16), preferred_element_type=f32)
        x_of = where(lax.broadcasted_iota(i32, (virt_count, count), 1))
        c_of = lax.broadcasted_iota(i32, (virt_count, count), 0)
        virt_part = jnp.dot(virt_rows, (c_of == starts + x_of % per).astype(bf16), preferred_element_type=f32)
        return jnp.bitwise_xor(occ_part.astype(i32), virt_part.astype(i32))[0:1, :]

    pair_count, rows_pair, block = shape
    per_row = rows_pair * pair_count // occ_count
    first = lax.axis_index("pair") * rows_pair
    for parity in range(2):
        row_ref[parity:parity + 1, :] = spread(
            rows_pair // 2, slab_ref[0], per_row,
            lambda x: first + ((x // block) * 2 + parity) * block + x % block)
    col_ref[...] = spread(cols, slab_ref[1], cols // occ_count)
    base = lax.axis_index("contr") * occ_local
    parts = [jnp.bitwise_xor(virt_v_ref[...].reshape(1, virt_count), occ_s_ref[base + k]) for k in range(occ_local)]
    kc_ref[...] = jnp.concatenate(parts, axis=1) if occ_local > 1 else parts[0]


def irreps(shape, slab_start, occ_irrep, virt_irrep, kc_local, cols):
    smem = pl.BlockSpec(memory_space=pltpu.SMEM)
    vmem = pl.BlockSpec(memory_space=pltpu.VMEM)
    shapes = [jax.ShapeDtypeStruct(n, jnp.int32) for n in ((2, shape[1] // 2), (1, kc_local), (1, cols))]
    return pl.pallas_call(
        functools.partial(_irrep_kernel, shape),
        out_shape=shapes,
        in_specs=[smem, smem, vmem, vmem],
        out_specs=[vmem, vmem, vmem],
    )(slab_start, occ_irrep, occ_irrep, virt_irrep)


def body(amplitudes, integrals, occ_irrep, virt_irrep, occ_energy, virt_energy, slab_start):
    pair_count = lax.axis_size("pair")
    contr_count = lax.axis_size("contr")
    pair_index = lax.axis_index("pair")
    contr_index = lax.axis_index("contr")
    virt_count = virt_irrep.shape[0]
    kc_local = integrals.shape[0]
    occ_local = kc_local // virt_count
    rows_pair = amplitudes.shape[0]
    cols_pair = integrals.shape[1]
    rows_device = rows_pair // contr_count
    slab_first = amplitudes.shape[0] * pair_count // occ_irrep.shape[0]
    slab_second = cols_pair * pair_count // occ_irrep.shape[0]
    first_start = slab_start[0]
    second_start = slab_start[1]
    a_energy = lax.dynamic_slice(virt_energy, (first_start,), (slab_first,))
    b_energy = lax.dynamic_slice(virt_energy, (second_start,), (slab_second,))
    row_energy = (occ_energy[:, None] - a_energy[None, :]).reshape(-1)
    col_energy = (occ_energy[:, None] - b_energy[None, :]).reshape(-1)
    zero = jnp.zeros((), jnp.bfloat16)
    whole_int = lax.all_gather(integrals, "pair", axis=1, tiled=True)
    block = rows_pair // contr_count
    split = contr_count & (contr_count - 1) == 0 and rows_pair % (2 * contr_count) == 0
    row_k, kc_k, col_k = irreps((pair_count, rows_pair, block if split else rows_pair // 2),
                                slab_start, occ_irrep, virt_irrep, kc_local, cols_pair * pair_count)
    kc_irrep = kc_k.reshape(-1)
    int_masked = jnp.where(kc_irrep[:, None] == col_k.reshape(-1)[None, :], whole_int, zero)

    def product(amp, irrep):
        masked = jnp.where(irrep[:, None] == kc_irrep[None, :], amp, zero)
        return jnp.dot(masked, int_masked, preferred_element_type=jnp.float32)

    if split:
        amp4 = amplitudes.reshape(rows_pair // (2 * block), 2, block, kc_local)
        core = contr_index % 2

        def half(parity):
            return product(amp4[:, parity].reshape(rows_pair // 2, kc_local), row_k[parity])

        sent = lax.cond(core == 0, lambda: half(1), lambda: half(0))
        summed = halving_scatter(sent, "contr", contr_count, contr_index, lambda: lax.optimization_barrier(
            lax.cond(core == 0, lambda: half(0), lambda: half(1))))
    else:
        partial = product(amplitudes, row_k.reshape(-1))
        summed = lax.psum_scatter(partial, "contr", scatter_dimension=0, tiled=True)
    mine_energy = lax.dynamic_slice(
        row_energy, (pair_index * rows_pair + contr_index * rows_device,), (rows_device,)
    )
    update = (summed / (mine_energy[:, None] + col_energy[None, :])).astype(jnp.bfloat16)
    return update


def solution(mesh):
    in_specs = (P("pair", "contr"), P("contr", "pair"), P(), P(), P(), P(), P())
    out_specs = P(("pair", "contr"), None)
    return jax.shard_map(body, mesh=mesh, in_specs=in_specs, out_specs=out_specs, check_vma=False)
```

```python
import functools

import jax
import jax.numpy as jnp
from jax import lax
from jax.experimental import pallas as pl
from jax.experimental.pallas import tpu as pltpu
from jax.sharding import PartitionSpec as P


def halving_scatter(partial, axis, count, index, second=None):
    rows, cols = partial.shape
    if second is not None:
        rows = 2 * rows
    block = rows // count
    bits = count.bit_length() - 1
    first = (index & 1) == 0

    def order(c):
        seq = list(range(bits))
        if c == 1 and bits >= 3:
            seq[1], seq[2] = seq[2], seq[1]
        return seq

    left = [list(range(bits - 1, -1, -1)) for _ in range(2)]
    stages = range(bits)
    if second is not None:
        got = lax.ppermute(partial, axis, [(i, i ^ 1) for i in range(count)])
        buf = (second() + got).reshape((2,) * (bits - 1) + (block, cols))
        left = [seq[:-1] for seq in left]
        stages = range(1, bits)
    else:
        buf = partial.reshape((2,) * bits + (block, cols))
    for stage in stages:
        split = [order(c)[stage] for c in range(2)]
        where = [left[c].index(split[c]) for c in range(2)]
        mine = [(index >> split[c]) & 1 for c in range(2)]
        if where[0] == where[1]:
            bit = jnp.where(first, mine[0], mine[1]) if split[0] != split[1] else mine[0]
            keep = lax.dynamic_index_in_dim(buf, bit, axis=where[0], keepdims=False)
            send = lax.dynamic_index_in_dim(buf, 1 - bit, axis=where[0], keepdims=False)
        else:
            picks = [
                [lax.dynamic_index_in_dim(buf, v, axis=where[c], keepdims=False)
                 for v in (mine[c], 1 - mine[c])]
                for c in range(2)
            ]
            keep = jnp.where(first, picks[0][0], picks[1][0])
            send = jnp.where(first, picks[0][1], picks[1][1])
        for c in range(2):
            left[c].pop(where[c])
        perm = [(i, i ^ (1 << order(i & 1)[stage])) for i in range(count)]
        buf = keep + lax.ppermute(send, axis, perm)
    return buf.reshape(block, cols)


def _irrep_kernel(shape, slab_ref, occ_s_ref, occ_v_ref, virt_v_ref, int_ref, row_ref, kc_ref, masked_ref):
    virt_count = virt_v_ref.shape[0]
    occ_count = occ_v_ref.shape[0]
    kc_local = kc_ref.shape[1]
    cols = int_ref.shape[1]
    occ_local = kc_local // virt_count
    f32, bf16, i32 = jnp.float32, jnp.bfloat16, jnp.int32
    occ_rows = jnp.broadcast_to(occ_v_ref[...].reshape(1, occ_count), (8, occ_count)).astype(bf16)
    virt_rows = jnp.broadcast_to(virt_v_ref[...].reshape(1, virt_count), (8, virt_count)).astype(bf16)

    def spread(count, starts, per, where=lambda x: x):
        x_of = where(lax.broadcasted_iota(i32, (occ_count, count), 1))
        j_of = lax.broadcasted_iota(i32, (occ_count, count), 0)
        occ_part = jnp.dot(occ_rows, (x_of // per == j_of).astype(bf16), preferred_element_type=f32)
        x_of = where(lax.broadcasted_iota(i32, (virt_count, count), 1))
        c_of = lax.broadcasted_iota(i32, (virt_count, count), 0)
        virt_part = jnp.dot(virt_rows, (c_of == starts + x_of % per).astype(bf16), preferred_element_type=f32)
        return jnp.bitwise_xor(occ_part.astype(i32), virt_part.astype(i32))[0:1, :]

    pair_count, rows_pair, block = shape
    per_row = rows_pair * pair_count // occ_count
    first = lax.axis_index("pair") * rows_pair
    for parity in range(2):
        row_ref[parity:parity + 1, :] = spread(
            rows_pair // 2, slab_ref[0], per_row,
            lambda x: first + ((x // block) * 2 + parity) * block + x % block)
    col_irrep = spread(cols, slab_ref[1], cols // occ_count)
    base = lax.axis_index("contr") * occ_local
    parts = [jnp.bitwise_xor(virt_v_ref[...].reshape(1, virt_count), occ_s_ref[base + k]) for k in range(occ_local)]
    kc_ref[...] = jnp.concatenate(parts, axis=1) if occ_local > 1 else parts[0]
    eye = (lax.broadcasted_iota(i32, (virt_count, virt_count), 0)
           == lax.broadcasted_iota(i32, (virt_count, virt_count), 1)).astype(bf16)
    virt_col = lax.dot_general(eye, virt_rows, (((1,), (1,)), ((), ())), preferred_element_type=f32)
    virt_col = virt_col.astype(i32)[:, 0:1]
    for k in range(occ_local):
        kc_col = jnp.bitwise_xor(virt_col, occ_s_ref[base + k])
        block = int_ref[k * virt_count:(k + 1) * virt_count, :]
        masked_ref[k * virt_count:(k + 1) * virt_count, :] = jnp.where(
            kc_col == col_irrep, block, jnp.zeros_like(block))


def irreps(shape, slab_start, occ_irrep, virt_irrep, integrals):
    smem = pl.BlockSpec(memory_space=pltpu.SMEM)
    vmem = pl.BlockSpec(memory_space=pltpu.VMEM)
    shapes = [jax.ShapeDtypeStruct((2, shape[1] // 2), jnp.int32),
              jax.ShapeDtypeStruct((1, integrals.shape[0]), jnp.int32),
              jax.ShapeDtypeStruct(integrals.shape, integrals.dtype)]
    return pl.pallas_call(
        functools.partial(_irrep_kernel, shape),
        out_shape=shapes,
        in_specs=[smem, smem, vmem, vmem, vmem],
        out_specs=[vmem, vmem, vmem],
    )(slab_start, occ_irrep, occ_irrep, virt_irrep, integrals)


def body(amplitudes, integrals, occ_irrep, virt_irrep, occ_energy, virt_energy, slab_start):
    pair_count = lax.axis_size("pair")
    contr_count = lax.axis_size("contr")
    pair_index = lax.axis_index("pair")
    contr_index = lax.axis_index("contr")
    virt_count = virt_irrep.shape[0]
    kc_local = integrals.shape[0]
    occ_local = kc_local // virt_count
    rows_pair = amplitudes.shape[0]
    cols_pair = integrals.shape[1]
    rows_device = rows_pair // contr_count
    slab_first = amplitudes.shape[0] * pair_count // occ_irrep.shape[0]
    slab_second = cols_pair * pair_count // occ_irrep.shape[0]
    first_start = slab_start[0]
    second_start = slab_start[1]
    a_energy = lax.dynamic_slice(virt_energy, (first_start,), (slab_first,))
    b_energy = lax.dynamic_slice(virt_energy, (second_start,), (slab_second,))
    row_energy = (occ_energy[:, None] - a_energy[None, :]).reshape(-1)
    col_energy = (occ_energy[:, None] - b_energy[None, :]).reshape(-1)
    zero = jnp.zeros((), jnp.bfloat16)
    whole_int = lax.all_gather(integrals, "pair", axis=1, tiled=True)
    block = rows_pair // contr_count
    split = contr_count & (contr_count - 1) == 0 and rows_pair % (2 * contr_count) == 0
    row_k, kc_k, int_masked = irreps((pair_count, rows_pair, block if split else rows_pair // 2),
                                     slab_start, occ_irrep, virt_irrep, whole_int)
    kc_irrep = kc_k.reshape(-1)

    def product(amp, irrep):
        masked = jnp.where(irrep[:, None] == kc_irrep[None, :], amp, zero)
        return jnp.dot(masked, int_masked, preferred_element_type=jnp.float32)

    if split:
        amp4 = amplitudes.reshape(rows_pair // (2 * block), 2, block, kc_local)
        core = contr_index % 2

        def half(parity):
            return product(amp4[:, parity].reshape(rows_pair // 2, kc_local), row_k[parity])

        sent = lax.cond(core == 0, lambda: half(1), lambda: half(0))
        summed = halving_scatter(sent, "contr", contr_count, contr_index, lambda: lax.optimization_barrier(
            lax.cond(core == 0, lambda: half(0), lambda: half(1))))
    else:
        partial = product(amplitudes, row_k.reshape(-1))
        summed = lax.psum_scatter(partial, "contr", scatter_dimension=0, tiled=True)
    mine_energy = lax.dynamic_slice(
        row_energy, (pair_index * rows_pair + contr_index * rows_device,), (rows_device,)
    )
    update = (summed / (mine_energy[:, None] + col_energy[None, :])).astype(jnp.bfloat16)
    return update


def solution(mesh):
    in_specs = (P("pair", "contr"), P("contr", "pair"), P(), P(), P(), P(), P())
    out_specs = P(("pair", "contr"), None)
    return jax.shard_map(body, mesh=mesh, in_specs=in_specs, out_specs=out_specs, check_vma=False)
```

```python
import functools

import jax
import jax.numpy as jnp
from jax import lax
from jax.experimental import pallas as pl
from jax.experimental.pallas import tpu as pltpu
from jax.sharding import PartitionSpec as P


def halving_scatter(partial, axis, count, index, second=None):
    rows, cols = partial.shape
    if second is not None:
        rows = 2 * rows
    block = rows // count
    bits = count.bit_length() - 1
    first = (index & 1) == 0

    def order(c):
        seq = list(range(bits))
        if c == 1 and bits >= 3:
            seq[1], seq[2] = seq[2], seq[1]
        return seq

    left = [list(range(bits - 1, -1, -1)) for _ in range(2)]
    stages = range(bits)
    if second is not None:
        got = lax.ppermute(partial, axis, [(i, i ^ 1) for i in range(count)])
        buf = (second() + got).reshape((2,) * (bits - 1) + (block, cols))
        left = [seq[:-1] for seq in left]
        stages = range(1, bits)
    else:
        buf = partial.reshape((2,) * bits + (block, cols))
    for stage in stages:
        split = [order(c)[stage] for c in range(2)]
        where = [left[c].index(split[c]) for c in range(2)]
        mine = [(index >> split[c]) & 1 for c in range(2)]
        if where[0] == where[1]:
            bit = jnp.where(first, mine[0], mine[1]) if split[0] != split[1] else mine[0]
            keep = lax.dynamic_index_in_dim(buf, bit, axis=where[0], keepdims=False)
            send = lax.dynamic_index_in_dim(buf, 1 - bit, axis=where[0], keepdims=False)
        else:
            picks = [
                [lax.dynamic_index_in_dim(buf, v, axis=where[c], keepdims=False)
                 for v in (mine[c], 1 - mine[c])]
                for c in range(2)
            ]
            keep = jnp.where(first, picks[0][0], picks[1][0])
            send = jnp.where(first, picks[0][1], picks[1][1])
        for c in range(2):
            left[c].pop(where[c])
        perm = [(i, i ^ (1 << order(i & 1)[stage])) for i in range(count)]
        buf = keep + lax.ppermute(send, axis, perm)
    return buf.reshape(block, cols)


def _irrep_kernel(shape, slab_ref, occ_s_ref, occ_v_ref, virt_v_ref, int_hbm, row_ref, kc_ref, masked_ref,
                  int_ref, sem):
    fetch = pltpu.make_async_copy(int_hbm, int_ref, sem)
    fetch.start()
    virt_count = virt_v_ref.shape[0]
    occ_count = occ_v_ref.shape[0]
    kc_local = kc_ref.shape[1]
    cols = int_ref.shape[1]
    occ_local = kc_local // virt_count
    f32, bf16, i32 = jnp.float32, jnp.bfloat16, jnp.int32
    occ_rows = jnp.broadcast_to(occ_v_ref[...].reshape(1, occ_count), (8, occ_count)).astype(bf16)
    virt_rows = jnp.broadcast_to(virt_v_ref[...].reshape(1, virt_count), (8, virt_count)).astype(bf16)

    def spread(count, starts, per, where=lambda x: x):
        x_of = where(lax.broadcasted_iota(i32, (occ_count, count), 1))
        j_of = lax.broadcasted_iota(i32, (occ_count, count), 0)
        occ_part = jnp.dot(occ_rows, (x_of // per == j_of).astype(bf16), preferred_element_type=f32)
        x_of = where(lax.broadcasted_iota(i32, (virt_count, count), 1))
        c_of = lax.broadcasted_iota(i32, (virt_count, count), 0)
        virt_part = jnp.dot(virt_rows, (c_of == starts + x_of % per).astype(bf16), preferred_element_type=f32)
        return jnp.bitwise_xor(occ_part.astype(i32), virt_part.astype(i32))[0:1, :]

    pair_count, rows_pair, block = shape
    per_row = rows_pair * pair_count // occ_count
    first = lax.axis_index("pair") * rows_pair
    for parity in range(2):
        row_ref[parity:parity + 1, :] = spread(
            rows_pair // 2, slab_ref[0], per_row,
            lambda x: first + ((x // block) * 2 + parity) * block + x % block)
    col_irrep = spread(cols, slab_ref[1], cols // occ_count)
    base = lax.axis_index("contr") * occ_local
    parts = [jnp.bitwise_xor(virt_v_ref[...].reshape(1, virt_count), occ_s_ref[base + k]) for k in range(occ_local)]
    kc_ref[...] = jnp.concatenate(parts, axis=1) if occ_local > 1 else parts[0]
    eye = (lax.broadcasted_iota(i32, (virt_count, virt_count), 0)
           == lax.broadcasted_iota(i32, (virt_count, virt_count), 1)).astype(bf16)
    virt_col = lax.dot_general(eye, virt_rows, (((1,), (1,)), ((), ())), preferred_element_type=f32)
    virt_col = virt_col.astype(i32)[:, 0:1]
    fetch.wait()
    for k in range(occ_local):
        kc_col = jnp.bitwise_xor(virt_col, occ_s_ref[base + k])
        block = int_ref[k * virt_count:(k + 1) * virt_count, :]
        masked_ref[k * virt_count:(k + 1) * virt_count, :] = jnp.where(
            kc_col == col_irrep, block, jnp.zeros_like(block))


def irreps(shape, slab_start, occ_irrep, virt_irrep, integrals):
    smem = pl.BlockSpec(memory_space=pltpu.SMEM)
    vmem = pl.BlockSpec(memory_space=pltpu.VMEM)
    shapes = [jax.ShapeDtypeStruct((2, shape[1] // 2), jnp.int32),
              jax.ShapeDtypeStruct((1, integrals.shape[0]), jnp.int32),
              jax.ShapeDtypeStruct(integrals.shape, integrals.dtype)]
    return pl.pallas_call(
        functools.partial(_irrep_kernel, shape),
        out_shape=shapes,
        in_specs=[smem, smem, vmem, vmem, pl.BlockSpec(memory_space=pl.ANY)],
        out_specs=[vmem, vmem, vmem],
        scratch_shapes=[pltpu.VMEM(integrals.shape, integrals.dtype), pltpu.SemaphoreType.DMA(())],
    )(slab_start, occ_irrep, occ_irrep, virt_irrep, integrals)


def body(amplitudes, integrals, occ_irrep, virt_irrep, occ_energy, virt_energy, slab_start):
    pair_count = lax.axis_size("pair")
    contr_count = lax.axis_size("contr")
    pair_index = lax.axis_index("pair")
    contr_index = lax.axis_index("contr")
    virt_count = virt_irrep.shape[0]
    kc_local = integrals.shape[0]
    occ_local = kc_local // virt_count
    rows_pair = amplitudes.shape[0]
    cols_pair = integrals.shape[1]
    rows_device = rows_pair // contr_count
    slab_first = amplitudes.shape[0] * pair_count // occ_irrep.shape[0]
    slab_second = cols_pair * pair_count // occ_irrep.shape[0]
    first_start = slab_start[0]
    second_start = slab_start[1]
    a_energy = lax.dynamic_slice(virt_energy, (first_start,), (slab_first,))
    b_energy = lax.dynamic_slice(virt_energy, (second_start,), (slab_second,))
    row_energy = (occ_energy[:, None] - a_energy[None, :]).reshape(-1)
    col_energy = (occ_energy[:, None] - b_energy[None, :]).reshape(-1)
    zero = jnp.zeros((), jnp.bfloat16)
    whole_int = lax.all_gather(integrals, "pair", axis=1, tiled=True)
    block = rows_pair // contr_count
    split = contr_count & (contr_count - 1) == 0 and rows_pair % (2 * contr_count) == 0
    row_k, kc_k, int_masked = irreps((pair_count, rows_pair, block if split else rows_pair // 2),
                                     slab_start, occ_irrep, virt_irrep, whole_int)
    kc_irrep = kc_k.reshape(-1)

    def product(amp, irrep):
        masked = jnp.where(irrep[:, None] == kc_irrep[None, :], amp, zero)
        return jnp.dot(masked, int_masked, preferred_element_type=jnp.float32)

    if split:
        amp4 = amplitudes.reshape(rows_pair // (2 * block), 2, block, kc_local)
        core = contr_index % 2

        def half(parity):
            return product(amp4[:, parity].reshape(rows_pair // 2, kc_local), row_k[parity])

        sent = lax.cond(core == 0, lambda: half(1), lambda: half(0))
        summed = halving_scatter(sent, "contr", contr_count, contr_index, lambda: lax.optimization_barrier(
            lax.cond(core == 0, lambda: half(0), lambda: half(1))))
    else:
        partial = product(amplitudes, row_k.reshape(-1))
        summed = lax.psum_scatter(partial, "contr", scatter_dimension=0, tiled=True)
    mine_energy = lax.dynamic_slice(
        row_energy, (pair_index * rows_pair + contr_index * rows_device,), (rows_device,)
    )
    update = (summed / (mine_energy[:, None] + col_energy[None, :])).astype(jnp.bfloat16)
    return update


def solution(mesh):
    in_specs = (P("pair", "contr"), P("contr", "pair"), P(), P(), P(), P(), P())
    out_specs = P(("pair", "contr"), None)
    return jax.shard_map(body, mesh=mesh, in_specs=in_specs, out_specs=out_specs, check_vma=False)
```

```python
import functools

import jax
import jax.numpy as jnp
from jax import lax
from jax.experimental import pallas as pl
from jax.experimental.pallas import tpu as pltpu
from jax.sharding import PartitionSpec as P


def halving_scatter(partial, axis, count, index, second=None):
    rows, cols = partial.shape
    if second is not None:
        rows = 2 * rows
    block = rows // count
    bits = count.bit_length() - 1
    first = (index & 1) == 0

    def order(c):
        seq = list(range(bits))
        return seq

    left = [list(range(bits - 1, -1, -1)) for _ in range(2)]
    stages = range(bits)
    if second is not None:
        got = lax.ppermute(partial, axis, [(i, i ^ 1) for i in range(count)])
        buf = (second() + got).reshape((2,) * (bits - 1) + (block, cols))
        left = [seq[:-1] for seq in left]
        stages = range(1, bits)
    else:
        buf = partial.reshape((2,) * bits + (block, cols))
    for stage in stages:
        split = [order(c)[stage] for c in range(2)]
        where = [left[c].index(split[c]) for c in range(2)]
        mine = [(index >> split[c]) & 1 for c in range(2)]
        if where[0] == where[1]:
            bit = jnp.where(first, mine[0], mine[1]) if split[0] != split[1] else mine[0]
            keep = lax.dynamic_index_in_dim(buf, bit, axis=where[0], keepdims=False)
            send = lax.dynamic_index_in_dim(buf, 1 - bit, axis=where[0], keepdims=False)
        else:
            picks = [
                [lax.dynamic_index_in_dim(buf, v, axis=where[c], keepdims=False)
                 for v in (mine[c], 1 - mine[c])]
                for c in range(2)
            ]
            keep = jnp.where(first, picks[0][0], picks[1][0])
            send = jnp.where(first, picks[0][1], picks[1][1])
        for c in range(2):
            left[c].pop(where[c])
        perm = [(i, i ^ (1 << order(i & 1)[stage])) for i in range(count)]
        buf = keep + lax.ppermute(send, axis, perm)
    return buf.reshape(block, cols)


def _irrep_kernel(shape, slab_ref, occ_s_ref, occ_v_ref, virt_v_ref, int_ref, row_ref, kc_ref, masked_ref):
    virt_count = virt_v_ref.shape[0]
    occ_count = occ_v_ref.shape[0]
    kc_local = kc_ref.shape[1]
    cols = int_ref.shape[1]
    occ_local = kc_local // virt_count
    f32, bf16, i32 = jnp.float32, jnp.bfloat16, jnp.int32
    occ_rows = jnp.broadcast_to(occ_v_ref[...].reshape(1, occ_count), (8, occ_count)).astype(bf16)
    virt_rows = jnp.broadcast_to(virt_v_ref[...].reshape(1, virt_count), (8, virt_count)).astype(bf16)

    def spread(count, starts, per, where=lambda x: x):
        x_of = where(lax.broadcasted_iota(i32, (occ_count, count), 1))
        j_of = lax.broadcasted_iota(i32, (occ_count, count), 0)
        occ_part = jnp.dot(occ_rows, (x_of // per == j_of).astype(bf16), preferred_element_type=f32)
        x_of = where(lax.broadcasted_iota(i32, (virt_count, count), 1))
        c_of = lax.broadcasted_iota(i32, (virt_count, count), 0)
        virt_part = jnp.dot(virt_rows, (c_of == starts + x_of % per).astype(bf16), preferred_element_type=f32)
        return jnp.bitwise_xor(occ_part.astype(i32), virt_part.astype(i32))[0:1, :]

    pair_count, rows_pair, block = shape
    per_row = rows_pair * pair_count // occ_count
    first = lax.axis_index("pair") * rows_pair
    for parity in range(2):
        row_ref[parity:parity + 1, :] = spread(
            rows_pair // 2, slab_ref[0], per_row,
            lambda x: first + ((x // block) * 2 + parity) * block + x % block)
    col_irrep = spread(cols, slab_ref[1], cols // occ_count)
    base = lax.axis_index("contr") * occ_local
    parts = [jnp.bitwise_xor(virt_v_ref[...].reshape(1, virt_count), occ_s_ref[base + k]) for k in range(occ_local)]
    kc_ref[...] = jnp.concatenate(parts, axis=1) if occ_local > 1 else parts[0]
    eye = (lax.broadcasted_iota(i32, (virt_count, virt_count), 0)
           == lax.broadcasted_iota(i32, (virt_count, virt_count), 1)).astype(bf16)
    virt_col = lax.dot_general(eye, virt_rows, (((1,), (1,)), ((), ())), preferred_element_type=f32)
    virt_col = virt_col.astype(i32)[:, 0:1]
    for k in range(occ_local):
        kc_col = jnp.bitwise_xor(virt_col, occ_s_ref[base + k])
        block = int_ref[k * virt_count:(k + 1) * virt_count, :]
        masked_ref[k * virt_count:(k + 1) * virt_count, :] = jnp.where(
            kc_col == col_irrep, block, jnp.zeros_like(block))


def irreps(shape, slab_start, occ_irrep, virt_irrep, integrals):
    smem = pl.BlockSpec(memory_space=pltpu.SMEM)
    vmem = pl.BlockSpec(memory_space=pltpu.VMEM)
    shapes = [jax.ShapeDtypeStruct((2, shape[1] // 2), jnp.int32),
              jax.ShapeDtypeStruct((1, integrals.shape[0]), jnp.int32),
              jax.ShapeDtypeStruct(integrals.shape, integrals.dtype)]
    return pl.pallas_call(
        functools.partial(_irrep_kernel, shape),
        out_shape=shapes,
        in_specs=[smem, smem, vmem, vmem, vmem],
        out_specs=[vmem, vmem, vmem],
    )(slab_start, occ_irrep, occ_irrep, virt_irrep, integrals)


def body(amplitudes, integrals, occ_irrep, virt_irrep, occ_energy, virt_energy, slab_start):
    pair_count = lax.axis_size("pair")
    contr_count = lax.axis_size("contr")
    pair_index = lax.axis_index("pair")
    contr_index = lax.axis_index("contr")
    virt_count = virt_irrep.shape[0]
    kc_local = integrals.shape[0]
    occ_local = kc_local // virt_count
    rows_pair = amplitudes.shape[0]
    cols_pair = integrals.shape[1]
    rows_device = rows_pair // contr_count
    slab_first = amplitudes.shape[0] * pair_count // occ_irrep.shape[0]
    slab_second = cols_pair * pair_count // occ_irrep.shape[0]
    first_start = slab_start[0]
    second_start = slab_start[1]
    a_energy = lax.dynamic_slice(virt_energy, (first_start,), (slab_first,))
    b_energy = lax.dynamic_slice(virt_energy, (second_start,), (slab_second,))
    row_energy = (occ_energy[:, None] - a_energy[None, :]).reshape(-1)
    col_energy = (occ_energy[:, None] - b_energy[None, :]).reshape(-1)
    zero = jnp.zeros((), jnp.bfloat16)
    whole_int = lax.all_gather(integrals, "pair", axis=1, tiled=True)
    block = rows_pair // contr_count
    split = contr_count & (contr_count - 1) == 0 and rows_pair % (2 * contr_count) == 0
    row_k, kc_k, int_masked = irreps((pair_count, rows_pair, block if split else rows_pair // 2),
                                     slab_start, occ_irrep, virt_irrep, whole_int)
    kc_irrep = kc_k.reshape(-1)

    def product(amp, irrep):
        masked = jnp.where(irrep[:, None] == kc_irrep[None, :], amp, zero)
        return jnp.dot(masked, int_masked, preferred_element_type=jnp.float32)

    if split:
        amp4 = amplitudes.reshape(rows_pair // (2 * block), 2, block, kc_local)
        core = contr_index % 2

        def half(parity):
            return product(amp4[:, parity].reshape(rows_pair // 2, kc_local), row_k[parity])

        sent = lax.cond(core == 0, lambda: half(1), lambda: half(0))
        summed = halving_scatter(sent, "contr", contr_count, contr_index, lambda: lax.optimization_barrier(
            lax.cond(core == 0, lambda: half(0), lambda: half(1))))
    else:
        partial = product(amplitudes, row_k.reshape(-1))
        summed = lax.psum_scatter(partial, "contr", scatter_dimension=0, tiled=True)
    mine_energy = lax.dynamic_slice(
        row_energy, (pair_index * rows_pair + contr_index * rows_device,), (rows_device,)
    )
    update = (summed / (mine_energy[:, None] + col_energy[None, :])).astype(jnp.bfloat16)
    return update


def solution(mesh):
    in_specs = (P("pair", "contr"), P("contr", "pair"), P(), P(), P(), P(), P())
    out_specs = P(("pair", "contr"), None)
    return jax.shard_map(body, mesh=mesh, in_specs=in_specs, out_specs=out_specs, check_vma=False)
```

```python
import functools

import jax
import jax.numpy as jnp
from jax import lax
from jax.experimental import pallas as pl
from jax.experimental.pallas import tpu as pltpu
from jax.sharding import PartitionSpec as P


def halving_scatter(partial, axis, count, index, second=None):
    rows, cols = partial.shape
    if second is not None:
        rows = 2 * rows
    block = rows // count
    bits = count.bit_length() - 1
    first = (index & 1) == 0

    def order(c):
        seq = list(range(bits))
        if c == 1 and bits >= 5:
            seq[1:4] = [3, 1, 2]
        elif c == 1 and bits >= 3:
            seq[1], seq[2] = seq[2], seq[1]
        return seq

    left = [list(range(bits - 1, -1, -1)) for _ in range(2)]
    stages = range(bits)
    if second is not None:
        got = lax.ppermute(partial, axis, [(i, i ^ 1) for i in range(count)])
        buf = (second() + got).reshape((2,) * (bits - 1) + (block, cols))
        left = [seq[:-1] for seq in left]
        stages = range(1, bits)
    else:
        buf = partial.reshape((2,) * bits + (block, cols))
    for stage in stages:
        split = [order(c)[stage] for c in range(2)]
        where = [left[c].index(split[c]) for c in range(2)]
        mine = [(index >> split[c]) & 1 for c in range(2)]
        if where[0] == where[1]:
            bit = jnp.where(first, mine[0], mine[1]) if split[0] != split[1] else mine[0]
            keep = lax.dynamic_index_in_dim(buf, bit, axis=where[0], keepdims=False)
            send = lax.dynamic_index_in_dim(buf, 1 - bit, axis=where[0], keepdims=False)
        else:
            picks = [
                [lax.dynamic_index_in_dim(buf, v, axis=where[c], keepdims=False)
                 for v in (mine[c], 1 - mine[c])]
                for c in range(2)
            ]
            keep = jnp.where(first, picks[0][0], picks[1][0])
            send = jnp.where(first, picks[0][1], picks[1][1])
        for c in range(2):
            left[c].pop(where[c])
        perm = [(i, i ^ (1 << order(i & 1)[stage])) for i in range(count)]
        buf = keep + lax.ppermute(send, axis, perm)
    return buf.reshape(block, cols)


def _irrep_kernel(shape, slab_ref, occ_s_ref, occ_v_ref, virt_v_ref, int_ref, row_ref, kc_ref, masked_ref):
    virt_count = virt_v_ref.shape[0]
    occ_count = occ_v_ref.shape[0]
    kc_local = kc_ref.shape[1]
    cols = int_ref.shape[1]
    occ_local = kc_local // virt_count
    f32, bf16, i32 = jnp.float32, jnp.bfloat16, jnp.int32
    occ_rows = jnp.broadcast_to(occ_v_ref[...].reshape(1, occ_count), (8, occ_count)).astype(bf16)
    virt_rows = jnp.broadcast_to(virt_v_ref[...].reshape(1, virt_count), (8, virt_count)).astype(bf16)

    def spread(count, starts, per, where=lambda x: x):
        x_of = where(lax.broadcasted_iota(i32, (occ_count, count), 1))
        j_of = lax.broadcasted_iota(i32, (occ_count, count), 0)
        occ_part = jnp.dot(occ_rows, (x_of // per == j_of).astype(bf16), preferred_element_type=f32)
        x_of = where(lax.broadcasted_iota(i32, (virt_count, count), 1))
        c_of = lax.broadcasted_iota(i32, (virt_count, count), 0)
        virt_part = jnp.dot(virt_rows, (c_of == starts + x_of % per).astype(bf16), preferred_element_type=f32)
        return jnp.bitwise_xor(occ_part.astype(i32), virt_part.astype(i32))[0:1, :]

    pair_count, rows_pair, block = shape
    per_row = rows_pair * pair_count // occ_count
    first = lax.axis_index("pair") * rows_pair
    for parity in range(2):
        row_ref[parity:parity + 1, :] = spread(
            rows_pair // 2, slab_ref[0], per_row,
            lambda x: first + ((x // block) * 2 + parity) * block + x % block)
    col_irrep = spread(cols, slab_ref[1], cols // occ_count)
    base = lax.axis_index("contr") * occ_local
    parts = [jnp.bitwise_xor(virt_v_ref[...].reshape(1, virt_count), occ_s_ref[base + k]) for k in range(occ_local)]
    kc_ref[...] = jnp.concatenate(parts, axis=1) if occ_local > 1 else parts[0]
    eye = (lax.broadcasted_iota(i32, (virt_count, virt_count), 0)
           == lax.broadcasted_iota(i32, (virt_count, virt_count), 1)).astype(bf16)
    virt_col = lax.dot_general(eye, virt_rows, (((1,), (1,)), ((), ())), preferred_element_type=f32)
    virt_col = virt_col.astype(i32)[:, 0:1]
    for k in range(occ_local):
        kc_col = jnp.bitwise_xor(virt_col, occ_s_ref[base + k])
        block = int_ref[k * virt_count:(k + 1) * virt_count, :]
        masked_ref[k * virt_count:(k + 1) * virt_count, :] = jnp.where(
            kc_col == col_irrep, block, jnp.zeros_like(block))


def irreps(shape, slab_start, occ_irrep, virt_irrep, integrals):
    smem = pl.BlockSpec(memory_space=pltpu.SMEM)
    vmem = pl.BlockSpec(memory_space=pltpu.VMEM)
    shapes = [jax.ShapeDtypeStruct((2, shape[1] // 2), jnp.int32),
              jax.ShapeDtypeStruct((1, integrals.shape[0]), jnp.int32),
              jax.ShapeDtypeStruct(integrals.shape, integrals.dtype)]
    return pl.pallas_call(
        functools.partial(_irrep_kernel, shape),
        out_shape=shapes,
        in_specs=[smem, smem, vmem, vmem, vmem],
        out_specs=[vmem, vmem, vmem],
    )(slab_start, occ_irrep, occ_irrep, virt_irrep, integrals)


def body(amplitudes, integrals, occ_irrep, virt_irrep, occ_energy, virt_energy, slab_start):
    pair_count = lax.axis_size("pair")
    contr_count = lax.axis_size("contr")
    pair_index = lax.axis_index("pair")
    contr_index = lax.axis_index("contr")
    virt_count = virt_irrep.shape[0]
    kc_local = integrals.shape[0]
    occ_local = kc_local // virt_count
    rows_pair = amplitudes.shape[0]
    cols_pair = integrals.shape[1]
    rows_device = rows_pair // contr_count
    slab_first = amplitudes.shape[0] * pair_count // occ_irrep.shape[0]
    slab_second = cols_pair * pair_count // occ_irrep.shape[0]
    first_start = slab_start[0]
    second_start = slab_start[1]
    a_energy = lax.dynamic_slice(virt_energy, (first_start,), (slab_first,))
    b_energy = lax.dynamic_slice(virt_energy, (second_start,), (slab_second,))
    row_energy = (occ_energy[:, None] - a_energy[None, :]).reshape(-1)
    col_energy = (occ_energy[:, None] - b_energy[None, :]).reshape(-1)
    zero = jnp.zeros((), jnp.bfloat16)
    whole_int = lax.all_gather(integrals, "pair", axis=1, tiled=True)
    block = rows_pair // contr_count
    split = contr_count & (contr_count - 1) == 0 and rows_pair % (2 * contr_count) == 0
    row_k, kc_k, int_masked = irreps((pair_count, rows_pair, block if split else rows_pair // 2),
                                     slab_start, occ_irrep, virt_irrep, whole_int)
    kc_irrep = kc_k.reshape(-1)

    def product(amp, irrep):
        masked = jnp.where(irrep[:, None] == kc_irrep[None, :], amp, zero)
        return jnp.dot(masked, int_masked, preferred_element_type=jnp.float32)

    if split:
        amp4 = amplitudes.reshape(rows_pair // (2 * block), 2, block, kc_local)
        core = contr_index % 2

        def half(parity):
            return product(amp4[:, parity].reshape(rows_pair // 2, kc_local), row_k[parity])

        sent = lax.cond(core == 0, lambda: half(1), lambda: half(0))
        summed = halving_scatter(sent, "contr", contr_count, contr_index, lambda: lax.optimization_barrier(
            lax.cond(core == 0, lambda: half(0), lambda: half(1))))
    else:
        partial = product(amplitudes, row_k.reshape(-1))
        summed = lax.psum_scatter(partial, "contr", scatter_dimension=0, tiled=True)
    mine_energy = lax.dynamic_slice(
        row_energy, (pair_index * rows_pair + contr_index * rows_device,), (rows_device,)
    )
    update = (summed / (mine_energy[:, None] + col_energy[None, :])).astype(jnp.bfloat16)
    return update


def solution(mesh):
    in_specs = (P("pair", "contr"), P("contr", "pair"), P(), P(), P(), P(), P())
    out_specs = P(("pair", "contr"), None)
    return jax.shard_map(body, mesh=mesh, in_specs=in_specs, out_specs=out_specs, check_vma=False)
```

```python
import functools

import jax
import jax.numpy as jnp
from jax import lax
from jax.experimental import pallas as pl
from jax.experimental.pallas import tpu as pltpu
from jax.sharding import PartitionSpec as P


def halving_scatter(partial, axis, count, index, second=None):
    rows, cols = partial.shape
    if second is not None:
        rows = 2 * rows
    block = rows // count
    bits = count.bit_length() - 1
    first = (index & 1) == 0

    def order(c):
        seq = list(range(bits))
        if c == 1 and bits >= 5:
            seq[1:4] = [2, 3, 1]
        elif c == 1 and bits >= 3:
            seq[1], seq[2] = seq[2], seq[1]
        return seq

    left = [list(range(bits - 1, -1, -1)) for _ in range(2)]
    stages = range(bits)
    if second is not None:
        got = lax.ppermute(partial, axis, [(i, i ^ 1) for i in range(count)])
        buf = (second() + got).reshape((2,) * (bits - 1) + (block, cols))
        left = [seq[:-1] for seq in left]
        stages = range(1, bits)
    else:
        buf = partial.reshape((2,) * bits + (block, cols))
    for stage in stages:
        split = [order(c)[stage] for c in range(2)]
        where = [left[c].index(split[c]) for c in range(2)]
        mine = [(index >> split[c]) & 1 for c in range(2)]
        if where[0] == where[1]:
            bit = jnp.where(first, mine[0], mine[1]) if split[0] != split[1] else mine[0]
            keep = lax.dynamic_index_in_dim(buf, bit, axis=where[0], keepdims=False)
            send = lax.dynamic_index_in_dim(buf, 1 - bit, axis=where[0], keepdims=False)
        else:
            picks = [
                [lax.dynamic_index_in_dim(buf, v, axis=where[c], keepdims=False)
                 for v in (mine[c], 1 - mine[c])]
                for c in range(2)
            ]
            keep = jnp.where(first, picks[0][0], picks[1][0])
            send = jnp.where(first, picks[0][1], picks[1][1])
        for c in range(2):
            left[c].pop(where[c])
        perm = [(i, i ^ (1 << order(i & 1)[stage])) for i in range(count)]
        buf = keep + lax.ppermute(send, axis, perm)
    return buf.reshape(block, cols)


def _irrep_kernel(shape, slab_ref, occ_s_ref, occ_v_ref, virt_v_ref, int_ref, row_ref, kc_ref, masked_ref):
    virt_count = virt_v_ref.shape[0]
    occ_count = occ_v_ref.shape[0]
    kc_local = kc_ref.shape[1]
    cols = int_ref.shape[1]
    occ_local = kc_local // virt_count
    f32, bf16, i32 = jnp.float32, jnp.bfloat16, jnp.int32
    occ_rows = jnp.broadcast_to(occ_v_ref[...].reshape(1, occ_count), (8, occ_count)).astype(bf16)
    virt_rows = jnp.broadcast_to(virt_v_ref[...].reshape(1, virt_count), (8, virt_count)).astype(bf16)

    def spread(count, starts, per, where=lambda x: x):
        x_of = where(lax.broadcasted_iota(i32, (occ_count, count), 1))
        j_of = lax.broadcasted_iota(i32, (occ_count, count), 0)
        occ_part = jnp.dot(occ_rows, (x_of // per == j_of).astype(bf16), preferred_element_type=f32)
        x_of = where(lax.broadcasted_iota(i32, (virt_count, count), 1))
        c_of = lax.broadcasted_iota(i32, (virt_count, count), 0)
        virt_part = jnp.dot(virt_rows, (c_of == starts + x_of % per).astype(bf16), preferred_element_type=f32)
        return jnp.bitwise_xor(occ_part.astype(i32), virt_part.astype(i32))[0:1, :]

    pair_count, rows_pair, block = shape
    per_row = rows_pair * pair_count // occ_count
    first = lax.axis_index("pair") * rows_pair
    for parity in range(2):
        row_ref[parity:parity + 1, :] = spread(
            rows_pair // 2, slab_ref[0], per_row,
            lambda x: first + ((x // block) * 2 + parity) * block + x % block)
    col_irrep = spread(cols, slab_ref[1], cols // occ_count)
    base = lax.axis_index("contr") * occ_local
    parts = [jnp.bitwise_xor(virt_v_ref[...].reshape(1, virt_count), occ_s_ref[base + k]) for k in range(occ_local)]
    kc_ref[...] = jnp.concatenate(parts, axis=1) if occ_local > 1 else parts[0]
    eye = (lax.broadcasted_iota(i32, (virt_count, virt_count), 0)
           == lax.broadcasted_iota(i32, (virt_count, virt_count), 1)).astype(bf16)
    virt_col = lax.dot_general(eye, virt_rows, (((1,), (1,)), ((), ())), preferred_element_type=f32)
    virt_col = virt_col.astype(i32)[:, 0:1]
    for k in range(occ_local):
        kc_col = jnp.bitwise_xor(virt_col, occ_s_ref[base + k])
        block = int_ref[k * virt_count:(k + 1) * virt_count, :]
        masked_ref[k * virt_count:(k + 1) * virt_count, :] = jnp.where(
            kc_col == col_irrep, block, jnp.zeros_like(block))


def irreps(shape, slab_start, occ_irrep, virt_irrep, integrals):
    smem = pl.BlockSpec(memory_space=pltpu.SMEM)
    vmem = pl.BlockSpec(memory_space=pltpu.VMEM)
    shapes = [jax.ShapeDtypeStruct((2, shape[1] // 2), jnp.int32),
              jax.ShapeDtypeStruct((1, integrals.shape[0]), jnp.int32),
              jax.ShapeDtypeStruct(integrals.shape, integrals.dtype)]
    return pl.pallas_call(
        functools.partial(_irrep_kernel, shape),
        out_shape=shapes,
        in_specs=[smem, smem, vmem, vmem, vmem],
        out_specs=[vmem, vmem, vmem],
    )(slab_start, occ_irrep, occ_irrep, virt_irrep, integrals)


def body(amplitudes, integrals, occ_irrep, virt_irrep, occ_energy, virt_energy, slab_start):
    pair_count = lax.axis_size("pair")
    contr_count = lax.axis_size("contr")
    pair_index = lax.axis_index("pair")
    contr_index = lax.axis_index("contr")
    virt_count = virt_irrep.shape[0]
    kc_local = integrals.shape[0]
    occ_local = kc_local // virt_count
    rows_pair = amplitudes.shape[0]
    cols_pair = integrals.shape[1]
    rows_device = rows_pair // contr_count
    slab_first = amplitudes.shape[0] * pair_count // occ_irrep.shape[0]
    slab_second = cols_pair * pair_count // occ_irrep.shape[0]
    first_start = slab_start[0]
    second_start = slab_start[1]
    a_energy = lax.dynamic_slice(virt_energy, (first_start,), (slab_first,))
    b_energy = lax.dynamic_slice(virt_energy, (second_start,), (slab_second,))
    row_energy = (occ_energy[:, None] - a_energy[None, :]).reshape(-1)
    col_energy = (occ_energy[:, None] - b_energy[None, :]).reshape(-1)
    zero = jnp.zeros((), jnp.bfloat16)
    whole_int = lax.all_gather(integrals, "pair", axis=1, tiled=True)
    block = rows_pair // contr_count
    split = contr_count & (contr_count - 1) == 0 and rows_pair % (2 * contr_count) == 0
    row_k, kc_k, int_masked = irreps((pair_count, rows_pair, block if split else rows_pair // 2),
                                     slab_start, occ_irrep, virt_irrep, whole_int)
    kc_irrep = kc_k.reshape(-1)

    def product(amp, irrep):
        masked = jnp.where(irrep[:, None] == kc_irrep[None, :], amp, zero)
        return jnp.dot(masked, int_masked, preferred_element_type=jnp.float32)

    if split:
        amp4 = amplitudes.reshape(rows_pair // (2 * block), 2, block, kc_local)
        core = contr_index % 2

        def half(parity):
            return product(amp4[:, parity].reshape(rows_pair // 2, kc_local), row_k[parity])

        sent = lax.cond(core == 0, lambda: half(1), lambda: half(0))
        summed = halving_scatter(sent, "contr", contr_count, contr_index, lambda: lax.optimization_barrier(
            lax.cond(core == 0, lambda: half(0), lambda: half(1))))
    else:
        partial = product(amplitudes, row_k.reshape(-1))
        summed = lax.psum_scatter(partial, "contr", scatter_dimension=0, tiled=True)
    mine_energy = lax.dynamic_slice(
        row_energy, (pair_index * rows_pair + contr_index * rows_device,), (rows_device,)
    )
    update = (summed / (mine_energy[:, None] + col_energy[None, :])).astype(jnp.bfloat16)
    return update


def solution(mesh):
    in_specs = (P("pair", "contr"), P("contr", "pair"), P(), P(), P(), P(), P())
    out_specs = P(("pair", "contr"), None)
    return jax.shard_map(body, mesh=mesh, in_specs=in_specs, out_specs=out_specs, check_vma=False)
```
